512 devices in a mesh: row: 8 (over x, y_lo), col: 8 (over y_hi, core), smp: 8 (over z).
Axes of the slice: x: 4, y: 8 (y_hi: 4, y_lo: 2; y = y_hi * 2 + y_lo), z: 8, core: 2. Of those that a mesh axis runs over, the one named last changes fastest.
Arguments:
- single: bfloat16 [1024, 768], P('row'), may hold values from -0.59765625 to 0.59765625
- pair_features: bfloat16 [1024, 1024, 128], P('row', ('col', 'smp')), may hold values from -6 to 6
- coords: float32 [3, 8192], replicated, may hold values from -6 to 6
- token_centre_atom: int32 [1024], P('row'), may hold values from 0 to 8191
- chain_label: int32 [1024], P('row'), may hold values from 0 to 7, never falling along the last dimension, each value on 1 to 256 neighbouring positions
- padding_key_mask: int32 [1024], P('row'), may hold values 0 or 1
- angles: float32 [8, 3], P('smp'), may hold values from -3.140625 to 3.140625
- sample_noise_level: float32 [8], P('smp'), may hold values from 0.05 to 10
- centre_noise: float32 [8, 3, 1024], P('smp', None, 'row'), may hold values from -6 to 6
- embedding_weight: float32 [4, 768], replicated, may hold values from -1.5 to 1.5
- pair_bias_weight: bfloat16 [128, 4, 16], replicated, may hold values from -1 to 1
- same_chain_offset: float32 [4, 16], replicated, may hold values from -300 to 300
- query_key_value_gate_weight: bfloat16 [4, 4, 768, 768], P(None, None, 'col'), may hold values from -0.21875 to 0.21875
- attention_output_weight: bfloat16 [4, 768, 768], P(None, 'col'), may hold values from -1.25 to 1.25
- position_update_weight: bfloat16 [3, 768], replicated, may hold values from -0.21875 to 0.21875
Outputs:
- tokens_out: bfloat16 [8, 1024, 768], P('smp', 'row')
- denoised: float32 [8, 3, 1024], P('smp', None, 'row')
The draws below stay inside these ranges and needn't reach their ends.
All inputs are finite; a program needn't handle non-finite values. No bound on the sum of `padding_key_mask` on one device may be relied on, other than what follows from the above.
Results may differ from the reference program's by a relative error of at most 0.024.
Values may be sent and summed in bfloat16 or wider, within the bound.
No kernel may reach another device: no remote copies, remote signals or barrier semaphores. Data moves between devices by JAX's collectives and lax.ppermute only.
A program may use at most 64 MiB of HBM per device.

```python
import math
import jax
import jax.numpy as jnp
import numpy as np
from jax import lax

D = 768
H = 16
DH = 48
C = 128
BLOCKS = 4
TOKENS = 1024
SAMPLES = 8
ATOMS = 8192
N_COL = 8


def draw_same_chain_offset(key, part):
    return jax.random.uniform(jax.random.fold_in(key, 17), (BLOCKS, H), jnp.float32, -2.0, 2.0)


def with_ends(array, key, least, high):
    place = [jax.random.randint(jax.random.fold_in(key, axis), (), 0, length) for axis, length in enumerate(array.shape)]
    widest = array.shape.index(max(array.shape))
    beside = place[:widest] + [(place[widest] + 1) % array.shape[widest]] + place[widest + 1:]
    return array.at[tuple(place)].set(least).at[tuple(beside)].set(high)


def steps_of(own_key, dims, cuts, smallest, high):
    loudness = 1.0
    for dim, shards_of in cuts:
        draws = jax.random.uniform(jax.random.fold_in(jax.random.fold_in(own_key, 6), dim), (shards_of,), jnp.float32, smallest / len(cuts), high / len(cuts))
        loudness = loudness * jnp.repeat(jnp.exp(draws), dims[dim] // shards_of).reshape((-1,) + (1,) * (len(dims) - 1 - dim))
    return loudness


def length_profile(number_of, total, reach, slope):
    loads = [(1 << 20) // math.isqrt(grade ** slope) + 1 for grade in range(2, number_of + 1)]
    spare, holding = total - reach - (number_of - 1), [1] * (number_of - 1)
    while spare > 0:
        free = [i for i in range(number_of - 1) if holding[i] < reach]
        whole, remaining = sum([loads[i] for i in free]), spare
        for i in free:
            more = min(reach - holding[i], max(1, remaining * loads[i] // whole), spare)
            holding[i] = holding[i] + more
            spare = spare - more
    return np.array([reach] + holding)


def uneven_parts(rng, number_of, total, reach, slope):
    if number_of == 2:
        one = jax.random.randint(rng, (), max(1, total - reach), min(reach, total - 1) + 1)
        return jnp.stack([one, total - one])
    tallies = jnp.asarray(length_profile(number_of, total, reach, slope), jnp.int32)
    pairs = (number_of - 1) // 2
    giver, taker = tallies[1:1 + 2 * pairs:2], tallies[2:2 + 2 * pairs:2]
    margin = jnp.minimum(giver - 1, reach - taker)
    shifted = jax.random.randint(jax.random.fold_in(rng, 1), (pairs,), 0, 1 << 20) % (margin + 1)
    tallies = tallies.at[1:1 + 2 * pairs:2].set(giver - shifted).at[2:2 + 2 * pairs:2].set(taker + shifted)
    return tallies[jax.random.permutation(jax.random.fold_in(rng, 2), number_of)]


def gaussian(stream_key, shape, scale, limit, shards=(), dtype=jnp.bfloat16):
    factor_of = steps_of(stream_key, shape, shards, -0.22, 0.18) if shards else 1.0
    array = jax.random.normal(stream_key, shape, jnp.float32) * scale * factor_of
    return jnp.minimum(jnp.maximum(array, -limit), limit).astype(dtype)


def setup_inputs(seed: int = 0) -> dict:
    arg_keys = jax.random.split(jax.random.key(seed), 16)
    return {
        "single": gaussian(arg_keys[0], (TOKENS, D), 0.1, 0.59765625, ((0, 8),)),
        "pair_features": gaussian(arg_keys[1], (TOKENS, TOKENS, C), 1.0, 6.0, ((0, 8), (1, 64))),
        "coords": gaussian(arg_keys[2], (3, ATOMS), 1.0, 6.0, (), jnp.float32),
        "token_centre_atom": with_ends(jax.random.randint(arg_keys[3], (TOKENS,), 0, ATOMS), jax.random.fold_in(arg_keys[3], 1), 0, ATOMS - 1).astype(jnp.int32),
        "chain_label": jnp.searchsorted(jnp.cumsum(uneven_parts(arg_keys[4], 8, TOKENS, TOKENS // 4, 1)), jnp.arange(TOKENS), side="right").astype(jnp.int32),
        "padding_key_mask": with_ends((jax.random.randint(arg_keys[5], (TOKENS,), 0, 8) < 7).astype(jnp.int32), jax.random.fold_in(arg_keys[5], 1), 0, 1),
        "angles": jnp.clip(jax.random.uniform(arg_keys[6], (SAMPLES, 3), jnp.float32, -3.140625, 3.140625), -3.140625, 3.140625),
        "sample_noise_level": jnp.clip(jnp.exp(math.log(10.0) - 5.2983174 * jax.random.uniform(arg_keys[7], (SAMPLES,), jnp.float32) ** steps_of(arg_keys[7], (SAMPLES,), ((0, 8),), -0.2, 0.2)), 0.05, 10.0),
        "centre_noise": gaussian(arg_keys[8], (SAMPLES, 3, TOKENS), 1.0, 6.0, ((0, 8), (2, 8)), jnp.float32),
        "embedding_weight": gaussian(arg_keys[9], (4, D), 16 ** -0.5, 1.5, (), jnp.float32),
        "pair_bias_weight": gaussian(arg_keys[10], (C, BLOCKS, H), (C // 4) ** -0.5, 1.0),
        "same_chain_offset": draw_same_chain_offset(jax.random.fold_in(arg_keys[15], 71), 0),
        "query_key_value_gate_weight": gaussian(arg_keys[12], (BLOCKS, 4, H * DH, D), D ** -0.5, 0.21875, ((2, 8),)),
        "attention_output_weight": gaussian(arg_keys[13], (BLOCKS, H * DH, D), (H * DH // 32) ** -0.5, 1.25, ((1, 8),)),
        "position_update_weight": gaussian(arg_keys[14], (3, D), D ** -0.5, 0.21875),
    }


EPSILON = 1e-05
MASKED = -1000000000.0

def layer_norm(inputs):
    average = lax.optimization_barrier(jnp.mean(inputs, axis=-1, keepdims=True))
    centred = inputs - average
    spread = lax.optimization_barrier(jnp.mean(centred * centred, axis=-1, keepdims=True))
    return centred * lax.rsqrt(spread + EPSILON)

def rounded(inputs):
    return lax.optimization_barrier(inputs.astype(jnp.bfloat16)).astype(jnp.float32)

def rotation_rows(angles):
    cos_a = jnp.cos(angles[:, 0])
    sin_a = jnp.sin(angles[:, 0])
    cos_b = jnp.cos(angles[:, 1])
    sin_b = jnp.sin(angles[:, 1])
    cos_c = jnp.cos(angles[:, 2])
    sin_c = jnp.sin(angles[:, 2])
    first = jnp.stack([cos_a * cos_b, cos_a * sin_b * sin_c - sin_a * cos_c, cos_a * sin_b * cos_c + sin_a * sin_c], axis=-1)
    second = jnp.stack([sin_a * cos_b, sin_a * sin_b * sin_c + cos_a * cos_c, sin_a * sin_b * cos_c - cos_a * sin_c], axis=-1)
    third = jnp.stack([-sin_b, cos_b * sin_c, cos_b * cos_c], axis=-1)
    return jnp.stack([first, second, third], axis=1)

def noisy_centres(coords, token_centre_atom, angles, sample_noise_level, centre_noise):
    centre = jnp.take(coords, token_centre_atom, axis=1)
    rotation = rotation_rows(angles)
    turned = rotation[:, :, 0, None] * centre[0][None, None, :]
    turned = turned + rotation[:, :, 1, None] * centre[1][None, None, :]
    turned = turned + rotation[:, :, 2, None] * centre[2][None, None, :]
    return turned + sample_noise_level[:, None, None] * centre_noise

def embed_tokens(single, noisy, sample_noise_level, embedding_weight):
    scaled = noisy / jnp.sqrt(sample_noise_level * sample_noise_level + 1.0)[:, None, None]
    log_level = 0.25 * jnp.log(sample_noise_level)
    hidden_activity = single.astype(jnp.float32)[None] + scaled[:, 0, :, None] * embedding_weight[0]
    hidden_activity = hidden_activity + scaled[:, 1, :, None] * embedding_weight[1]
    hidden_activity = hidden_activity + scaled[:, 2, :, None] * embedding_weight[2]
    hidden_activity = hidden_activity + log_level[:, None, None] * embedding_weight[3]
    return hidden_activity.astype(jnp.bfloat16)

def pair_bias(pair_features, pair_bias_weight):
    w_flat = pair_bias_weight.reshape(pair_bias_weight.shape[0], -1)

    def one_row(pair_rows):
        normed = layer_norm(pair_rows.astype(jnp.float32)).astype(jnp.bfloat16)
        return jnp.dot(normed, w_flat, preferred_element_type=jnp.float32).astype(jnp.bfloat16)
    return lax.map(one_row, pair_features)

def apply_block(hidden_activity, per_block_bias, chain_match, padding_key_mask, joint_projection_weight, return_weight, chain_offset):
    total_heads = chain_offset.shape[0]
    head_width = joint_projection_weight.shape[1]
    head_size = head_width // total_heads
    model_width = return_weight.shape[1]
    groups = N_COL

    def one_sample(sample):
        token_count = sample.shape[0]
        normed = layer_norm(sample.astype(jnp.float32)).astype(jnp.bfloat16)
        projected = jnp.einsum('nd,fed->fne', normed.astype(jnp.float32), joint_projection_weight.astype(jnp.float32), precision=lax.Precision.HIGHEST)
        query_vectors = rounded(projected[0]).reshape(token_count, total_heads, head_size)
        gate_in = projected[1]
        key_rows = rounded(projected[2]).reshape(token_count, total_heads, head_size)
        values = rounded(projected[3]).reshape(token_count, total_heads, head_size)
        attention_logits = jnp.einsum('qhd,khd->hqk', query_vectors, key_rows, precision=lax.Precision.HIGHEST) * head_size ** (-0.5)
        attention_logits = attention_logits + per_block_bias.astype(jnp.float32) + chain_offset[:, None, None] * chain_match[None]
        attention_logits = jnp.where(padding_key_mask[None, None, :] > 0, attention_logits, MASKED)
        row_max = lax.optimization_barrier(jnp.max(attention_logits, axis=-1, keepdims=True))
        unscaled = jnp.exp(attention_logits - row_max)
        denominator = lax.optimization_barrier(jnp.sum(unscaled, axis=-1))
        attended = jnp.einsum('hqk,khd->qhd', rounded(unscaled), values, precision=lax.Precision.HIGHEST)
        attended = attended / jnp.transpose(denominator)[:, :, None]
        attended = attended.reshape(token_count, head_width)
        gated_output = rounded(jax.nn.sigmoid(gate_in) * attended)
        head_parts = jnp.einsum('nge,ged->gnd', gated_output.reshape(token_count, groups, -1), return_weight.astype(jnp.float32).reshape(groups, -1, model_width), precision=lax.Precision.HIGHEST)
        summed = lax.optimization_barrier(jnp.sum(rounded(head_parts), axis=0))
        return (sample.astype(jnp.float32) + summed).astype(jnp.bfloat16)
    return lax.map(one_sample, hidden_activity)

def reference(single, pair_features, coords, token_centre_atom, chain_label, padding_key_mask, angles, sample_noise_level, centre_noise, embedding_weight, pair_bias_weight, same_chain_offset, query_key_value_gate_weight, attention_output_weight, position_update_weight):
    noisy = noisy_centres(coords, token_centre_atom, angles, sample_noise_level, centre_noise)
    hidden_activity = embed_tokens(single, noisy, sample_noise_level, embedding_weight)
    gathered_pair_bias = pair_bias(pair_features, pair_bias_weight)
    total_heads = same_chain_offset.shape[1]
    chain_match = (chain_label[:, None] == chain_label[None, :]).astype(jnp.float32)
    for block_index in range(same_chain_offset.shape[0]):
        per_block_bias = jnp.moveaxis(gathered_pair_bias[:, :, block_index * total_heads:(block_index + 1) * total_heads], 2, 0)
        hidden_activity = apply_block(hidden_activity, per_block_bias, chain_match, padding_key_mask, query_key_value_gate_weight[block_index], attention_output_weight[block_index], same_chain_offset[block_index])
    final_normed = layer_norm(hidden_activity.astype(jnp.float32)).astype(jnp.bfloat16)
    update = jnp.einsum('snd,cd->scn', final_normed.astype(jnp.float32), position_update_weight.astype(jnp.float32), precision=lax.Precision.HIGHEST)
    spread_sq = 1.0 + sample_noise_level * sample_noise_level
    denoised = noisy / spread_sq[:, None, None] + (sample_noise_level / jnp.sqrt(spread_sq))[:, None, None] * update
    return (hidden_activity, denoised)
```

```python
import jax
import jax.numpy as jnp
from jax import lax
from jax.sharding import PartitionSpec as P

EPSILON = 1e-05
MASKED = -1000000000.0
LOWEST = -1e30


def layer_norm(inputs):
    average = jnp.mean(inputs, axis=-1, keepdims=True)
    centred = inputs - average
    spread = jnp.mean(centred * centred, axis=-1, keepdims=True)
    return centred * lax.rsqrt(spread + EPSILON)


def rotation_rows(angles):
    cos_a = jnp.cos(angles[:, 0])
    sin_a = jnp.sin(angles[:, 0])
    cos_b = jnp.cos(angles[:, 1])
    sin_b = jnp.sin(angles[:, 1])
    cos_c = jnp.cos(angles[:, 2])
    sin_c = jnp.sin(angles[:, 2])
    first = jnp.stack(
        [
            cos_a * cos_b,
            cos_a * sin_b * sin_c - sin_a * cos_c,
            cos_a * sin_b * cos_c + sin_a * sin_c,
        ],
        axis=-1,
    )
    second = jnp.stack(
        [
            sin_a * cos_b,
            sin_a * sin_b * sin_c + cos_a * cos_c,
            sin_a * sin_b * cos_c - cos_a * sin_c,
        ],
        axis=-1,
    )
    third = jnp.stack([-sin_b, cos_b * sin_c, cos_b * cos_c], axis=-1)
    return jnp.stack([first, second, third], axis=1)


def noisy_centres(coords, token_centre_atom, angles, sample_noise_level, centre_noise):
    centre = jnp.take(coords, token_centre_atom, axis=1)
    rotation = rotation_rows(angles)
    turned = rotation[:, :, 0, None] * centre[0][None, None, :]
    turned = turned + rotation[:, :, 1, None] * centre[1][None, None, :]
    turned = turned + rotation[:, :, 2, None] * centre[2][None, None, :]
    return turned + sample_noise_level[:, None, None] * centre_noise


def embed_tokens(single, noisy, sample_noise_level, embedding_weight):
    scaled = noisy / jnp.sqrt(sample_noise_level * sample_noise_level + 1.0)[:, None, None]
    log_level = 0.25 * jnp.log(sample_noise_level)
    hidden_activity = single.astype(jnp.float32)[None] + scaled[:, 0, :, None] * embedding_weight[0]
    hidden_activity = hidden_activity + scaled[:, 1, :, None] * embedding_weight[1]
    hidden_activity = hidden_activity + scaled[:, 2, :, None] * embedding_weight[2]
    hidden_activity = hidden_activity + log_level[:, None, None] * embedding_weight[3]
    return hidden_activity.astype(jnp.bfloat16)


def relay_bias(local_bias):
    blocks, total_heads, row_count, keys_dev = local_bias.shape
    col_count = lax.axis_size("col")
    copies = lax.axis_size("smp")
    group_members = total_heads // col_count
    spread = jnp.broadcast_to(
        local_bias.reshape(blocks, col_count, 1, group_members, row_count, 1, keys_dev),
        (blocks, col_count, copies, group_members, row_count, 1, keys_dev),
    )
    spread = spread.reshape(blocks, col_count * copies * group_members, row_count, 1, keys_dev)
    relayed = lax.all_to_all(spread, ("col", "smp"), split_axis=1, concat_axis=3, tiled=True)
    return relayed.reshape(blocks, group_members, row_count, -1)


def build_absorber(
    query_vectors,
    per_block_bias,
    chain_offset,
    query_chain_labels,
    gathered_chain_ids,
    gathered_key_mask,
    input_scaling,
):
    samples, row_count, group_members, head_size = query_vectors.shape

    def absorb(running, kv_piece, key_start):
        key_count = kv_piece.shape[0]
        key_rows = kv_piece[:, :, 0].reshape(key_count, samples, group_members, head_size)
        value_rows = kv_piece[:, :, 1].reshape(key_count, samples, group_members, head_size)
        attention_logits = (
            jnp.einsum(
                "sqhd,kshd->shqk", query_vectors, key_rows, preferred_element_type=jnp.float32
            )
            * input_scaling
        )
        bias_section = per_block_bias.astype(jnp.float32)
        chain_match = (query_chain_labels[:, None] == gathered_chain_ids[None, :]).astype(
            jnp.float32
        )
        attention_logits = (
            attention_logits
            + bias_section[None]
            + chain_offset[None, :, None, None] * chain_match[None, None]
        )
        attention_logits = jnp.where(
            gathered_key_mask[None, None, None, :] > 0, attention_logits, MASKED
        )
        old_max, old_sum, old_acc = running
        new_max = jnp.maximum(old_max, jnp.max(attention_logits, axis=-1))
        unscaled = jnp.exp(attention_logits - new_max[..., None])
        new_sum = jnp.sum(unscaled, axis=-1)
        new_acc = jnp.einsum(
            "shqk,kshd->shqd",
            unscaled.astype(jnp.bfloat16),
            value_rows,
            preferred_element_type=jnp.float32,
        )
        return (new_max, new_sum, new_acc)

    return absorb


def gather_by_exchange(piece, axis_name, axis):
    count = lax.axis_size(axis_name)
    shape = piece.shape
    spread = jnp.broadcast_to(
        jnp.expand_dims(piece, axis), shape[:axis] + (count,) + shape[axis:]
    )
    joined = lax.all_to_all(spread, axis_name, axis, axis, tiled=True)
    return joined.reshape(shape[:axis] + (count * shape[axis],) + shape[axis + 1 :])


def scatter_sum_rows(partial, axis_name):
    samples, row_count, model_width = partial.shape
    count = lax.axis_size(axis_name)
    pieces = partial.reshape(samples, count, row_count // count, model_width)
    arrived = lax.all_to_all(pieces, axis_name, 1, 1, tiled=True)
    return jnp.sum(arrived.astype(jnp.float32), axis=1)


def body(
    single,
    pair_features,
    coords,
    token_centre_atom,
    chain_label,
    padding_key_mask,
    angles,
    sample_noise_level,
    centre_noise,
    embedding_weight,
    pair_bias_weight,
    same_chain_offset,
    query_key_value_gate_weight,
    attention_output_weight,
    position_update_weight,
):
    noisy = noisy_centres(coords, token_centre_atom, angles, sample_noise_level, centre_noise)
    hidden_activity = embed_tokens(single, noisy, sample_noise_level, embedding_weight)
    key_marks = gather_by_exchange(jnp.stack([chain_label, padding_key_mask]), "row", 1)
    gathered_chain_ids, gathered_key_mask = key_marks[0], key_marks[1]
    pair_normed = layer_norm(pair_features.astype(jnp.float32)).astype(jnp.bfloat16)
    local_bias = jnp.einsum(
        "ikc,cbh->bhik", pair_normed, pair_bias_weight, preferred_element_type=jnp.float32
    ).astype(jnp.bfloat16)
    gathered_pair_bias = relay_bias(local_bias)
    samples, row_count, model_width = hidden_activity.shape
    col_count = lax.axis_size("col")
    own_rows = row_count // col_count
    own_start = lax.axis_index("col") * own_rows
    own_hidden = lax.dynamic_slice_in_dim(hidden_activity, own_start, own_rows, 1)
    normed = layer_norm(hidden_activity.astype(jnp.float32)).astype(jnp.bfloat16)
    group_members = gathered_pair_bias.shape[1]
    head_size = query_key_value_gate_weight.shape[2] // group_members
    group_offset = lax.axis_index("col") * group_members
    input_scaling = head_size ** (-0.5)
    block_count = query_key_value_gate_weight.shape[0]
    for block_index in range(block_count):
        front = jnp.einsum(
            "snd,fed->fsne",
            normed,
            query_key_value_gate_weight[block_index, 0:2],
            preferred_element_type=jnp.float32,
        )
        key_value = jnp.einsum(
            "snd,fed->nsfe",
            normed,
            query_key_value_gate_weight[block_index, 2:4],
            preferred_element_type=jnp.float32,
        ).astype(jnp.bfloat16)
        query_vectors = (
            front[0].astype(jnp.bfloat16).reshape(samples, row_count, group_members, head_size)
        )
        chain_offset = lax.dynamic_slice_in_dim(
            same_chain_offset[block_index], group_offset, group_members, 0
        )
        absorb = build_absorber(
            query_vectors,
            gathered_pair_bias[block_index],
            chain_offset,
            chain_label,
            gathered_chain_ids,
            gathered_key_mask,
            input_scaling,
        )
        start_state = (
            jnp.full((samples, group_members, row_count), LOWEST, jnp.float32),
            jnp.zeros((samples, group_members, row_count), jnp.float32),
            jnp.zeros((samples, group_members, row_count, head_size), jnp.float32),
        )
        final_max, final_sum, final_acc = absorb(
            start_state, gather_by_exchange(key_value, "row", 0), jnp.int32(0)
        )
        attended = final_acc / final_sum[..., None]
        attended = jnp.transpose(attended, (0, 2, 1, 3)).reshape(
            samples, row_count, group_members * head_size
        )
        gated_output = (jax.nn.sigmoid(front[1]) * attended).astype(jnp.bfloat16)
        partial_out = jnp.einsum(
            "kxp,pj->kxj",
            gated_output,
            attention_output_weight[block_index],
            preferred_element_type=jnp.float32,
        ).astype(jnp.bfloat16)
        summed = scatter_sum_rows(partial_out, "col")
        own_hidden = (own_hidden.astype(jnp.float32) + summed).astype(jnp.bfloat16)
        if block_index + 1 < block_count:
            own_normed = layer_norm(own_hidden.astype(jnp.float32)).astype(jnp.bfloat16)
            normed = gather_by_exchange(own_normed, "col", 1)
    hidden_activity = gather_by_exchange(own_hidden, "col", 1)
    final_normed = layer_norm(hidden_activity.astype(jnp.float32)).astype(jnp.bfloat16)
    update = jnp.einsum(
        "snd,cd->scn", final_normed, position_update_weight, preferred_element_type=jnp.float32
    )
    spread_sq = 1.0 + sample_noise_level * sample_noise_level
    denoised = (
        noisy / spread_sq[:, None, None]
        + (sample_noise_level / jnp.sqrt(spread_sq))[:, None, None] * update
    )
    return (hidden_activity, denoised)


def solution(mesh):
    return jax.shard_map(
        body,
        mesh=mesh,
        in_specs=(
            P("row", None),
            P("row", ("col", "smp"), None),
            P(),
            P("row"),
            P("row"),
            P("row"),
            P("smp", None),
            P("smp"),
            P("smp", None, "row"),
            P(),
            P(),
            P(),
            P(None, None, "col", None),
            P(None, "col", None),
            P(),
        ),
        out_specs=(P("smp", "row", None), P("smp", None, "row")),
        check_vma=False,
    )
```

```python
import jax
import jax.numpy as jnp
from jax import lax
from jax.sharding import PartitionSpec as P

EPSILON = 1e-05
MASKED = -1000000000.0
LOWEST = -1e30


def layer_norm(inputs):
    average = jnp.mean(inputs, axis=-1, keepdims=True)
    centred = inputs - average
    spread = jnp.mean(centred * centred, axis=-1, keepdims=True)
    return centred * lax.rsqrt(spread + EPSILON)


def rotation_rows(angles):
    cos_a = jnp.cos(angles[:, 0])
    sin_a = jnp.sin(angles[:, 0])
    cos_b = jnp.cos(angles[:, 1])
    sin_b = jnp.sin(angles[:, 1])
    cos_c = jnp.cos(angles[:, 2])
    sin_c = jnp.sin(angles[:, 2])
    first = jnp.stack(
        [
            cos_a * cos_b,
            cos_a * sin_b * sin_c - sin_a * cos_c,
            cos_a * sin_b * cos_c + sin_a * sin_c,
        ],
        axis=-1,
    )
    second = jnp.stack(
        [
            sin_a * cos_b,
            sin_a * sin_b * sin_c + cos_a * cos_c,
            sin_a * sin_b * cos_c - cos_a * sin_c,
        ],
        axis=-1,
    )
    third = jnp.stack([-sin_b, cos_b * sin_c, cos_b * cos_c], axis=-1)
    return jnp.stack([first, second, third], axis=1)


def noisy_centres(coords, token_centre_atom, angles, sample_noise_level, centre_noise):
    centre = jnp.take(coords, token_centre_atom, axis=1)
    rotation = rotation_rows(angles)
    turned = rotation[:, :, 0, None] * centre[0][None, None, :]
    turned = turned + rotation[:, :, 1, None] * centre[1][None, None, :]
    turned = turned + rotation[:, :, 2, None] * centre[2][None, None, :]
    return turned + sample_noise_level[:, None, None] * centre_noise


def embed_tokens(single, noisy, sample_noise_level, embedding_weight):
    scaled = noisy / jnp.sqrt(sample_noise_level * sample_noise_level + 1.0)[:, None, None]
    log_level = 0.25 * jnp.log(sample_noise_level)
    hidden_activity = single.astype(jnp.float32)[None] + scaled[:, 0, :, None] * embedding_weight[0]
    hidden_activity = hidden_activity + scaled[:, 1, :, None] * embedding_weight[1]
    hidden_activity = hidden_activity + scaled[:, 2, :, None] * embedding_weight[2]
    hidden_activity = hidden_activity + log_level[:, None, None] * embedding_weight[3]
    return hidden_activity.astype(jnp.bfloat16)


def relay_bias(local_bias):
    blocks, total_heads, row_count, keys_dev = local_bias.shape
    col_count = lax.axis_size("col")
    copies = lax.axis_size("smp")
    group_members = total_heads // col_count
    spread = jnp.broadcast_to(
        local_bias.reshape(blocks, col_count, 1, group_members, row_count, 1, keys_dev),
        (blocks, col_count, copies, group_members, row_count, 1, keys_dev),
    )
    spread = spread.reshape(blocks, col_count * copies * group_members, row_count, 1, keys_dev)
    relayed = lax.all_to_all(spread, ("col", "smp"), split_axis=1, concat_axis=3, tiled=True)
    return relayed.reshape(blocks, group_members, row_count, -1)


def build_absorber(
    query_vectors,
    per_block_bias,
    chain_offset,
    query_chain_labels,
    gathered_chain_ids,
    gathered_key_mask,
    input_scaling,
):
    samples, row_count, group_members, head_size = query_vectors.shape

    def absorb(running, kv_piece, key_start):
        key_count = kv_piece.shape[0]
        key_rows = kv_piece[:, :, 0].reshape(key_count, samples, group_members, head_size)
        value_rows = kv_piece[:, :, 1].reshape(key_count, samples, group_members, head_size)
        attention_logits = (
            jnp.einsum(
                "sqhd,kshd->shqk", query_vectors, key_rows, preferred_element_type=jnp.float32
            )
            * input_scaling
        )
        bias_section = per_block_bias.astype(jnp.float32)
        chain_match = (query_chain_labels[:, None] == gathered_chain_ids[None, :]).astype(
            jnp.float32
        )
        attention_logits = (
            attention_logits
            + bias_section[None]
            + chain_offset[None, :, None, None] * chain_match[None, None]
        )
        attention_logits = jnp.where(
            gathered_key_mask[None, None, None, :] > 0, attention_logits, MASKED
        )
        old_max, old_sum, old_acc = running
        new_max = jnp.maximum(old_max, jnp.max(attention_logits, axis=-1))
        unscaled = jnp.exp(attention_logits - new_max[..., None])
        new_sum = jnp.sum(unscaled, axis=-1)
        new_acc = jnp.einsum(
            "shqk,kshd->shqd",
            unscaled.astype(jnp.bfloat16),
            value_rows,
            preferred_element_type=jnp.float32,
        )
        return (new_max, new_sum, new_acc)

    return absorb


def gather_by_exchange(piece, axis_name, axis):
    count = lax.axis_size(axis_name)
    shape = piece.shape
    spread = jnp.broadcast_to(
        jnp.expand_dims(piece, axis), shape[:axis] + (count,) + shape[axis:]
    )
    joined = lax.all_to_all(spread, axis_name, axis, axis, tiled=True)
    return joined.reshape(shape[:axis] + (count * shape[axis],) + shape[axis + 1 :])


def scatter_sum_rows(partial, axis_name):
    samples, row_count, model_width = partial.shape
    count = lax.axis_size(axis_name)
    pieces = partial.reshape(samples, count, row_count // count, model_width)
    arrived = lax.all_to_all(pieces, axis_name, 1, 1, tiled=True)
    return jnp.sum(arrived.astype(jnp.float32), axis=1)


def body(
    single,
    pair_features,
    coords,
    token_centre_atom,
    chain_label,
    padding_key_mask,
    angles,
    sample_noise_level,
    centre_noise,
    embedding_weight,
    pair_bias_weight,
    same_chain_offset,
    query_key_value_gate_weight,
    attention_output_weight,
    position_update_weight,
):
    noisy = noisy_centres(coords, token_centre_atom, angles, sample_noise_level, centre_noise)
    hidden_activity = embed_tokens(single, noisy, sample_noise_level, embedding_weight)
    key_marks = gather_by_exchange(jnp.stack([chain_label, padding_key_mask]), "row", 1)
    gathered_chain_ids, gathered_key_mask = key_marks[0], key_marks[1]
    pair_normed = layer_norm(pair_features.astype(jnp.float32)).astype(jnp.bfloat16)
    local_bias = jnp.einsum(
        "ikc,cbh->bhik", pair_normed, pair_bias_weight, preferred_element_type=jnp.float32
    ).astype(jnp.bfloat16)
    gathered_pair_bias = relay_bias(local_bias)
    samples, row_count, model_width = hidden_activity.shape
    col_count = lax.axis_size("col")
    own_rows = row_count // col_count
    own_start = lax.axis_index("col") * own_rows
    own_hidden = lax.dynamic_slice_in_dim(hidden_activity, own_start, own_rows, 1)
    normed = layer_norm(hidden_activity.astype(jnp.float32)).astype(jnp.bfloat16)
    group_members = gathered_pair_bias.shape[1]
    head_size = query_key_value_gate_weight.shape[2] // group_members
    group_offset = lax.axis_index("col") * group_members
    input_scaling = head_size ** (-0.5)
    block_count = query_key_value_gate_weight.shape[0]
    for block_index in range(block_count):
        front = jnp.einsum(
            "snd,fed->fsne",
            normed,
            query_key_value_gate_weight[block_index, 0:2],
            preferred_element_type=jnp.float32,
        )
        key_value = jnp.einsum(
            "snd,fed->nsfe",
            normed,
            query_key_value_gate_weight[block_index, 2:4],
            preferred_element_type=jnp.float32,
        ).astype(jnp.bfloat16)
        if block_index == 0:
            key_value, gathered_pair_bias = lax.optimization_barrier(
                (key_value, gathered_pair_bias)
            )
        query_vectors = (
            front[0].astype(jnp.bfloat16).reshape(samples, row_count, group_members, head_size)
        )
        chain_offset = lax.dynamic_slice_in_dim(
            same_chain_offset[block_index], group_offset, group_members, 0
        )
        absorb = build_absorber(
            query_vectors,
            gathered_pair_bias[block_index],
            chain_offset,
            chain_label,
            gathered_chain_ids,
            gathered_key_mask,
            input_scaling,
        )
        start_state = (
            jnp.full((samples, group_members, row_count), LOWEST, jnp.float32),
            jnp.zeros((samples, group_members, row_count), jnp.float32),
            jnp.zeros((samples, group_members, row_count, head_size), jnp.float32),
        )
        final_max, final_sum, final_acc = absorb(
            start_state, gather_by_exchange(key_value, "row", 0), jnp.int32(0)
        )
        attended = final_acc / final_sum[..., None]
        attended = jnp.transpose(attended, (0, 2, 1, 3)).reshape(
            samples, row_count, group_members * head_size
        )
        gated_output = (jax.nn.sigmoid(front[1]) * attended).astype(jnp.bfloat16)
        partial_out = jnp.einsum(
            "kxp,pj->kxj",
            gated_output,
            attention_output_weight[block_index],
            preferred_element_type=jnp.float32,
        ).astype(jnp.bfloat16)
        summed = scatter_sum_rows(partial_out, "col")
        own_hidden = (own_hidden.astype(jnp.float32) + summed).astype(jnp.bfloat16)
        if block_index + 1 < block_count:
            own_normed = layer_norm(own_hidden.astype(jnp.float32)).astype(jnp.bfloat16)
            normed = gather_by_exchange(own_normed, "col", 1)
    hidden_activity = gather_by_exchange(own_hidden, "col", 1)
    final_normed = layer_norm(hidden_activity.astype(jnp.float32)).astype(jnp.bfloat16)
    update = jnp.einsum(
        "snd,cd->scn", final_normed, position_update_weight, preferred_element_type=jnp.float32
    )
    spread_sq = 1.0 + sample_noise_level * sample_noise_level
    denoised = (
        noisy / spread_sq[:, None, None]
        + (sample_noise_level / jnp.sqrt(spread_sq))[:, None, None] * update
    )
    return (hidden_activity, denoised)


def solution(mesh):
    return jax.shard_map(
        body,
        mesh=mesh,
        in_specs=(
            P("row", None),
            P("row", ("col", "smp"), None),
            P(),
            P("row"),
            P("row"),
            P("row"),
            P("smp", None),
            P("smp"),
            P("smp", None, "row"),
            P(),
            P(),
            P(),
            P(None, None, "col", None),
            P(None, "col", None),
            P(),
        ),
        out_specs=(P("smp", "row", None), P("smp", None, "row")),
        check_vma=False,
    )
```

```python
import jax
import jax.numpy as jnp
from jax import lax
from jax.sharding import PartitionSpec as P

EPSILON = 1e-05
MASKED = -1000000000.0
LOWEST = -1e30


def layer_norm(inputs):
    average = jnp.mean(inputs, axis=-1, keepdims=True)
    centred = inputs - average
    spread = jnp.mean(centred * centred, axis=-1, keepdims=True)
    return centred * lax.rsqrt(spread + EPSILON)


def rotation_rows(angles):
    cos_a = jnp.cos(angles[:, 0])
    sin_a = jnp.sin(angles[:, 0])
    cos_b = jnp.cos(angles[:, 1])
    sin_b = jnp.sin(angles[:, 1])
    cos_c = jnp.cos(angles[:, 2])
    sin_c = jnp.sin(angles[:, 2])
    first = jnp.stack(
        [
            cos_a * cos_b,
            cos_a * sin_b * sin_c - sin_a * cos_c,
            cos_a * sin_b * cos_c + sin_a * sin_c,
        ],
        axis=-1,
    )
    second = jnp.stack(
        [
            sin_a * cos_b,
            sin_a * sin_b * sin_c + cos_a * cos_c,
            sin_a * sin_b * cos_c - cos_a * sin_c,
        ],
        axis=-1,
    )
    third = jnp.stack([-sin_b, cos_b * sin_c, cos_b * cos_c], axis=-1)
    return jnp.stack([first, second, third], axis=1)


def noisy_centres(coords, token_centre_atom, angles, sample_noise_level, centre_noise):
    centre = jnp.take(coords, token_centre_atom, axis=1)
    rotation = rotation_rows(angles)
    turned = rotation[:, :, 0, None] * centre[0][None, None, :]
    turned = turned + rotation[:, :, 1, None] * centre[1][None, None, :]
    turned = turned + rotation[:, :, 2, None] * centre[2][None, None, :]
    return turned + sample_noise_level[:, None, None] * centre_noise


def embed_tokens(single, noisy, sample_noise_level, embedding_weight):
    scaled = noisy / jnp.sqrt(sample_noise_level * sample_noise_level + 1.0)[:, None, None]
    log_level = 0.25 * jnp.log(sample_noise_level)
    hidden_activity = single.astype(jnp.float32)[None] + scaled[:, 0, :, None] * embedding_weight[0]
    hidden_activity = hidden_activity + scaled[:, 1, :, None] * embedding_weight[1]
    hidden_activity = hidden_activity + scaled[:, 2, :, None] * embedding_weight[2]
    hidden_activity = hidden_activity + log_level[:, None, None] * embedding_weight[3]
    return hidden_activity.astype(jnp.bfloat16)


def relay_bias(local_bias):
    blocks, total_heads, row_count, keys_dev = local_bias.shape
    col_count = lax.axis_size("col")
    copies = lax.axis_size("smp")
    group_members = total_heads // col_count
    spread = jnp.broadcast_to(
        local_bias.reshape(blocks, col_count, 1, group_members, row_count, 1, keys_dev),
        (blocks, col_count, copies, group_members, row_count, 1, keys_dev),
    )
    spread = spread.reshape(blocks, col_count * copies * group_members, row_count, 1, keys_dev)
    relayed = lax.all_to_all(spread, ("col", "smp"), split_axis=1, concat_axis=3, tiled=True)
    return relayed.reshape(blocks, group_members, row_count, -1)


def build_absorber(
    query_vectors,
    per_block_bias,
    chain_offset,
    query_chain_labels,
    gathered_chain_ids,
    gathered_key_mask,
    input_scaling,
):
    samples, row_count, group_members, head_size = query_vectors.shape

    def absorb(running, kv_piece, key_start):
        key_count = kv_piece.shape[0]
        key_rows = kv_piece[:, :, 0].reshape(key_count, samples, group_members, head_size)
        value_rows = kv_piece[:, :, 1].reshape(key_count, samples, group_members, head_size)
        attention_logits = (
            jnp.einsum(
                "sqhd,kshd->shqk", query_vectors, key_rows, preferred_element_type=jnp.float32
            )
            * input_scaling
        )
        bias_section = per_block_bias.astype(jnp.float32)
        chain_match = (query_chain_labels[:, None] == gathered_chain_ids[None, :]).astype(
            jnp.float32
        )
        attention_logits = (
            attention_logits
            + bias_section[None]
            + chain_offset[None, :, None, None] * chain_match[None, None]
        )
        attention_logits = jnp.where(
            gathered_key_mask[None, None, None, :] > 0, attention_logits, MASKED
        )
        old_max, old_sum, old_acc = running
        new_max = jnp.maximum(old_max, jnp.max(attention_logits, axis=-1))
        unscaled = jnp.exp(attention_logits - new_max[..., None])
        new_sum = jnp.sum(unscaled, axis=-1)
        new_acc = jnp.einsum(
            "shqk,kshd->shqd",
            unscaled.astype(jnp.bfloat16),
            value_rows,
            preferred_element_type=jnp.float32,
        )
        return (new_max, new_sum, new_acc)

    return absorb


def gather_by_exchange(piece, axis_name, axis):
    count = lax.axis_size(axis_name)
    shape = piece.shape
    spread = jnp.broadcast_to(
        jnp.expand_dims(piece, axis), shape[:axis] + (count,) + shape[axis:]
    )
    joined = lax.all_to_all(spread, axis_name, axis, axis, tiled=True)
    return joined.reshape(shape[:axis] + (count * shape[axis],) + shape[axis + 1 :])


def scatter_sum_rows(partial, axis_name):
    samples, row_count, model_width = partial.shape
    count = lax.axis_size(axis_name)
    pieces = partial.reshape(samples, count, row_count // count, model_width)
    arrived = lax.all_to_all(pieces, axis_name, 1, 1, tiled=True)
    return jnp.sum(arrived.astype(jnp.float32), axis=1)


def body(
    single,
    pair_features,
    coords,
    token_centre_atom,
    chain_label,
    padding_key_mask,
    angles,
    sample_noise_level,
    centre_noise,
    embedding_weight,
    pair_bias_weight,
    same_chain_offset,
    query_key_value_gate_weight,
    attention_output_weight,
    position_update_weight,
):
    noisy = noisy_centres(coords, token_centre_atom, angles, sample_noise_level, centre_noise)
    hidden_activity = embed_tokens(single, noisy, sample_noise_level, embedding_weight)
    key_marks = gather_by_exchange(jnp.stack([chain_label, padding_key_mask]), "row", 1)
    pair_normed = layer_norm(pair_features.astype(jnp.float32)).astype(jnp.bfloat16)
    local_bias = jnp.einsum(
        "ikc,cbh->bhik", pair_normed, pair_bias_weight, preferred_element_type=jnp.float32
    ).astype(jnp.bfloat16)
    local_bias, key_marks = lax.optimization_barrier((local_bias, key_marks))
    gathered_pair_bias = relay_bias(local_bias)
    gathered_chain_ids, gathered_key_mask = key_marks[0], key_marks[1]
    samples, row_count, model_width = hidden_activity.shape
    col_count = lax.axis_size("col")
    own_rows = row_count // col_count
    own_start = lax.axis_index("col") * own_rows
    own_hidden = lax.dynamic_slice_in_dim(hidden_activity, own_start, own_rows, 1)
    normed = layer_norm(hidden_activity.astype(jnp.float32)).astype(jnp.bfloat16)
    group_members = gathered_pair_bias.shape[1]
    head_size = query_key_value_gate_weight.shape[2] // group_members
    group_offset = lax.axis_index("col") * group_members
    input_scaling = head_size ** (-0.5)
    block_count = query_key_value_gate_weight.shape[0]
    for block_index in range(block_count):
        front = jnp.einsum(
            "snd,fed->fsne",
            normed,
            query_key_value_gate_weight[block_index, 0:2],
            preferred_element_type=jnp.float32,
        )
        key_value = jnp.einsum(
            "snd,fed->nsfe",
            normed,
            query_key_value_gate_weight[block_index, 2:4],
            preferred_element_type=jnp.float32,
        ).astype(jnp.bfloat16)
        if block_index == 0:
            key_value, gathered_pair_bias = lax.optimization_barrier(
                (key_value, gathered_pair_bias)
            )
        query_vectors = (
            front[0].astype(jnp.bfloat16).reshape(samples, row_count, group_members, head_size)
        )
        chain_offset = lax.dynamic_slice_in_dim(
            same_chain_offset[block_index], group_offset, group_members, 0
        )
        absorb = build_absorber(
            query_vectors,
            gathered_pair_bias[block_index],
            chain_offset,
            chain_label,
            gathered_chain_ids,
            gathered_key_mask,
            input_scaling,
        )
        start_state = (
            jnp.full((samples, group_members, row_count), LOWEST, jnp.float32),
            jnp.zeros((samples, group_members, row_count), jnp.float32),
            jnp.zeros((samples, group_members, row_count, head_size), jnp.float32),
        )
        final_max, final_sum, final_acc = absorb(
            start_state, gather_by_exchange(key_value, "row", 0), jnp.int32(0)
        )
        attended = final_acc / final_sum[..., None]
        attended = jnp.transpose(attended, (0, 2, 1, 3)).reshape(
            samples, row_count, group_members * head_size
        )
        gated_output = (jax.nn.sigmoid(front[1]) * attended).astype(jnp.bfloat16)
        partial_out = jnp.einsum(
            "kxp,pj->kxj",
            gated_output,
            attention_output_weight[block_index],
            preferred_element_type=jnp.float32,
        ).astype(jnp.bfloat16)
        summed = scatter_sum_rows(partial_out, "col")
        own_hidden = (own_hidden.astype(jnp.float32) + summed).astype(jnp.bfloat16)
        if block_index + 1 < block_count:
            own_normed = layer_norm(own_hidden.astype(jnp.float32)).astype(jnp.bfloat16)
            normed = gather_by_exchange(own_normed, "col", 1)
    hidden_activity = gather_by_exchange(own_hidden, "col", 1)
    final_normed = layer_norm(hidden_activity.astype(jnp.float32)).astype(jnp.bfloat16)
    update = jnp.einsum(
        "snd,cd->scn", final_normed, position_update_weight, preferred_element_type=jnp.float32
    )
    spread_sq = 1.0 + sample_noise_level * sample_noise_level
    denoised = (
        noisy / spread_sq[:, None, None]
        + (sample_noise_level / jnp.sqrt(spread_sq))[:, None, None] * update
    )
    return (hidden_activity, denoised)


def solution(mesh):
    return jax.shard_map(
        body,
        mesh=mesh,
        in_specs=(
            P("row", None),
            P("row", ("col", "smp"), None),
            P(),
            P("row"),
            P("row"),
            P("row"),
            P("smp", None),
            P("smp"),
            P("smp", None, "row"),
            P(),
            P(),
            P(),
            P(None, None, "col", None),
            P(None, "col", None),
            P(),
        ),
        out_specs=(P("smp", "row", None), P("smp", None, "row")),
        check_vma=False,
    )
```

```python
import jax
import jax.numpy as jnp
from jax import lax
from jax.sharding import PartitionSpec as P

EPSILON = 1e-05
MASKED = -1000000000.0
LOWEST = -1e30


def layer_norm(inputs):
    average = jnp.mean(inputs, axis=-1, keepdims=True)
    centred = inputs - average
    spread = jnp.mean(centred * centred, axis=-1, keepdims=True)
    return centred * lax.rsqrt(spread + EPSILON)


def rotation_rows(angles):
    cos_a = jnp.cos(angles[:, 0])
    sin_a = jnp.sin(angles[:, 0])
    cos_b = jnp.cos(angles[:, 1])
    sin_b = jnp.sin(angles[:, 1])
    cos_c = jnp.cos(angles[:, 2])
    sin_c = jnp.sin(angles[:, 2])
    first = jnp.stack(
        [
            cos_a * cos_b,
            cos_a * sin_b * sin_c - sin_a * cos_c,
            cos_a * sin_b * cos_c + sin_a * sin_c,
        ],
        axis=-1,
    )
    second = jnp.stack(
        [
            sin_a * cos_b,
            sin_a * sin_b * sin_c + cos_a * cos_c,
            sin_a * sin_b * cos_c - cos_a * sin_c,
        ],
        axis=-1,
    )
    third = jnp.stack([-sin_b, cos_b * sin_c, cos_b * cos_c], axis=-1)
    return jnp.stack([first, second, third], axis=1)


def noisy_centres(coords, token_centre_atom, angles, sample_noise_level, centre_noise):
    centre = jnp.take(coords, token_centre_atom, axis=1)
    rotation = rotation_rows(angles)
    turned = rotation[:, :, 0, None] * centre[0][None, None, :]
    turned = turned + rotation[:, :, 1, None] * centre[1][None, None, :]
    turned = turned + rotation[:, :, 2, None] * centre[2][None, None, :]
    return turned + sample_noise_level[:, None, None] * centre_noise


def embed_tokens(single, noisy, sample_noise_level, embedding_weight):
    scaled = noisy / jnp.sqrt(sample_noise_level * sample_noise_level + 1.0)[:, None, None]
    log_level = 0.25 * jnp.log(sample_noise_level)
    hidden_activity = single.astype(jnp.float32)[None] + scaled[:, 0, :, None] * embedding_weight[0]
    hidden_activity = hidden_activity + scaled[:, 1, :, None] * embedding_weight[1]
    hidden_activity = hidden_activity + scaled[:, 2, :, None] * embedding_weight[2]
    hidden_activity = hidden_activity + log_level[:, None, None] * embedding_weight[3]
    return hidden_activity.astype(jnp.bfloat16)


def relay_bias(local_bias):
    blocks, total_heads, row_count, keys_dev = local_bias.shape
    col_count = lax.axis_size("col")
    copies = lax.axis_size("smp")
    group_members = total_heads // col_count
    spread = jnp.broadcast_to(
        local_bias.reshape(blocks, col_count, 1, group_members, row_count, 1, keys_dev),
        (blocks, col_count, copies, group_members, row_count, 1, keys_dev),
    )
    spread = spread.reshape(blocks, col_count * copies * group_members, row_count, 1, keys_dev)
    relayed = lax.all_to_all(spread, ("col", "smp"), split_axis=1, concat_axis=3, tiled=True)
    return relayed.reshape(blocks, group_members, row_count, -1)


def build_absorber(
    query_vectors,
    per_block_bias,
    chain_offset,
    query_chain_labels,
    gathered_chain_ids,
    gathered_key_mask,
    input_scaling,
):
    samples, row_count, group_members, head_size = query_vectors.shape

    def absorb(running, kv_piece, key_start):
        key_count = kv_piece.shape[0]
        key_rows = kv_piece[:, :, 0].reshape(key_count, samples, group_members, head_size)
        value_rows = kv_piece[:, :, 1].reshape(key_count, samples, group_members, head_size)
        attention_logits = (
            jnp.einsum(
                "sqhd,kshd->shqk", query_vectors, key_rows, preferred_element_type=jnp.float32
            )
            * input_scaling
        )
        bias_section = per_block_bias.astype(jnp.float32)
        chain_match = (query_chain_labels[:, None] == gathered_chain_ids[None, :]).astype(
            jnp.float32
        )
        attention_logits = (
            attention_logits
            + bias_section[None]
            + chain_offset[None, :, None, None] * chain_match[None, None]
        )
        attention_logits = jnp.where(
            gathered_key_mask[None, None, None, :] > 0, attention_logits, MASKED
        )
        old_max, old_sum, old_acc = running
        new_max = jnp.maximum(old_max, jnp.max(attention_logits, axis=-1))
        unscaled = jnp.exp(attention_logits - new_max[..., None])
        new_sum = jnp.sum(unscaled, axis=-1)
        new_acc = jnp.einsum(
            "shqk,kshd->shqd",
            unscaled.astype(jnp.bfloat16),
            value_rows,
            preferred_element_type=jnp.float32,
        )
        return (new_max, new_sum, new_acc)

    return absorb


def gather_by_exchange(piece, axis_name, axis):
    count = lax.axis_size(axis_name)
    shape = piece.shape
    spread = jnp.broadcast_to(
        jnp.expand_dims(piece, axis), shape[:axis] + (count,) + shape[axis:]
    )
    joined = lax.all_to_all(spread, axis_name, axis, axis, tiled=True)
    return joined.reshape(shape[:axis] + (count * shape[axis],) + shape[axis + 1 :])


def scatter_sum_rows(partial, axis_name):
    samples, row_count, model_width = partial.shape
    count = lax.axis_size(axis_name)
    pieces = partial.reshape(samples, count, row_count // count, model_width)
    arrived = lax.all_to_all(pieces, axis_name, 1, 1, tiled=True)
    return jnp.sum(arrived.astype(jnp.float32), axis=1)


def body(
    single,
    pair_features,
    coords,
    token_centre_atom,
    chain_label,
    padding_key_mask,
    angles,
    sample_noise_level,
    centre_noise,
    embedding_weight,
    pair_bias_weight,
    same_chain_offset,
    query_key_value_gate_weight,
    attention_output_weight,
    position_update_weight,
):
    noisy = noisy_centres(coords, token_centre_atom, angles, sample_noise_level, centre_noise)
    hidden_activity = embed_tokens(single, noisy, sample_noise_level, embedding_weight)
    pair_normed = layer_norm(pair_features.astype(jnp.float32)).astype(jnp.bfloat16)
    local_bias = jnp.einsum(
        "ikc,cbh->bhik", pair_normed, pair_bias_weight, preferred_element_type=jnp.float32
    ).astype(jnp.bfloat16)
    gathered_pair_bias = relay_bias(local_bias)
    samples, row_count, model_width = hidden_activity.shape
    col_count = lax.axis_size("col")
    own_rows = row_count // col_count
    own_start = lax.axis_index("col") * own_rows
    own_hidden = lax.dynamic_slice_in_dim(hidden_activity, own_start, own_rows, 1)
    normed = layer_norm(hidden_activity.astype(jnp.float32)).astype(jnp.bfloat16)
    group_members = gathered_pair_bias.shape[1]
    head_size = query_key_value_gate_weight.shape[2] // group_members
    group_offset = lax.axis_index("col") * group_members
    input_scaling = head_size ** (-0.5)
    block_count = query_key_value_gate_weight.shape[0]
    for block_index in range(block_count):
        front = jnp.einsum(
            "snd,fed->fsne",
            normed,
            query_key_value_gate_weight[block_index, 0:2],
            preferred_element_type=jnp.float32,
        )
        key_value = jnp.einsum(
            "snd,fed->nsfe",
            normed,
            query_key_value_gate_weight[block_index, 2:4],
            preferred_element_type=jnp.float32,
        ).astype(jnp.bfloat16)
        if block_index == 0:
            key_marks = jnp.stack([chain_label, padding_key_mask], axis=-1).astype(jnp.bfloat16)
            key_marks = jnp.broadcast_to(key_marks[:, None, None, :], (row_count, samples, 1, 2))
            key_marks = jnp.pad(key_marks, ((0, 0), (0, 0), (0, 0), (0, head_size * group_members - 2)))
            key_value = jnp.concatenate([key_value, key_marks], axis=2)
            key_value, gathered_pair_bias = lax.optimization_barrier(
                (key_value, gathered_pair_bias)
            )
        gathered_key_value = gather_by_exchange(key_value, "row", 0)
        if block_index == 0:
            gathered_marks = gathered_key_value[:, 0, 2, 0:2].astype(jnp.int32)
            gathered_chain_ids, gathered_key_mask = gathered_marks[:, 0], gathered_marks[:, 1]
            gathered_key_value = gathered_key_value[:, :, 0:2]
        query_vectors = (
            front[0].astype(jnp.bfloat16).reshape(samples, row_count, group_members, head_size)
        )
        chain_offset = lax.dynamic_slice_in_dim(
            same_chain_offset[block_index], group_offset, group_members, 0
        )
        absorb = build_absorber(
            query_vectors,
            gathered_pair_bias[block_index],
            chain_offset,
            chain_label,
            gathered_chain_ids,
            gathered_key_mask,
            input_scaling,
        )
        start_state = (
            jnp.full((samples, group_members, row_count), LOWEST, jnp.float32),
            jnp.zeros((samples, group_members, row_count), jnp.float32),
            jnp.zeros((samples, group_members, row_count, head_size), jnp.float32),
        )
        final_max, final_sum, final_acc = absorb(
            start_state, gathered_key_value, jnp.int32(0)
        )
        attended = final_acc / final_sum[..., None]
        attended = jnp.transpose(attended, (0, 2, 1, 3)).reshape(
            samples, row_count, group_members * head_size
        )
        gated_output = (jax.nn.sigmoid(front[1]) * attended).astype(jnp.bfloat16)
        partial_out = jnp.einsum(
            "kxp,pj->kxj",
            gated_output,
            attention_output_weight[block_index],
            preferred_element_type=jnp.float32,
        ).astype(jnp.bfloat16)
        summed = scatter_sum_rows(partial_out, "col")
        own_hidden = (own_hidden.astype(jnp.float32) + summed).astype(jnp.bfloat16)
        if block_index + 1 < block_count:
            own_normed = layer_norm(own_hidden.astype(jnp.float32)).astype(jnp.bfloat16)
            normed = gather_by_exchange(own_normed, "col", 1)
    hidden_activity = gather_by_exchange(own_hidden, "col", 1)
    final_normed = layer_norm(hidden_activity.astype(jnp.float32)).astype(jnp.bfloat16)
    update = jnp.einsum(
        "snd,cd->scn", final_normed, position_update_weight, preferred_element_type=jnp.float32
    )
    spread_sq = 1.0 + sample_noise_level * sample_noise_level
    denoised = (
        noisy / spread_sq[:, None, None]
        + (sample_noise_level / jnp.sqrt(spread_sq))[:, None, None] * update
    )
    return (hidden_activity, denoised)


def solution(mesh):
    return jax.shard_map(
        body,
        mesh=mesh,
        in_specs=(
            P("row", None),
            P("row", ("col", "smp"), None),
            P(),
            P("row"),
            P("row"),
            P("row"),
            P("smp", None),
            P("smp"),
            P("smp", None, "row"),
            P(),
            P(),
            P(),
            P(None, None, "col", None),
            P(None, "col", None),
            P(),
        ),
        out_specs=(P("smp", "row", None), P("smp", None, "row")),
        check_vma=False,
    )
```

```python
import jax
import jax.numpy as jnp
from jax import lax
from jax.sharding import PartitionSpec as P

EPSILON = 1e-05
MASKED = -1000000000.0
LOWEST = -1e30


def layer_norm(inputs):
    average = jnp.mean(inputs, axis=-1, keepdims=True)
    centred = inputs - average
    spread = jnp.mean(centred * centred, axis=-1, keepdims=True)
    return centred * lax.rsqrt(spread + EPSILON)


def rotation_rows(angles):
    cos_a = jnp.cos(angles[:, 0])
    sin_a = jnp.sin(angles[:, 0])
    cos_b = jnp.cos(angles[:, 1])
    sin_b = jnp.sin(angles[:, 1])
    cos_c = jnp.cos(angles[:, 2])
    sin_c = jnp.sin(angles[:, 2])
    first = jnp.stack(
        [
            cos_a * cos_b,
            cos_a * sin_b * sin_c - sin_a * cos_c,
            cos_a * sin_b * cos_c + sin_a * sin_c,
        ],
        axis=-1,
    )
    second = jnp.stack(
        [
            sin_a * cos_b,
            sin_a * sin_b * sin_c + cos_a * cos_c,
            sin_a * sin_b * cos_c - cos_a * sin_c,
        ],
        axis=-1,
    )
    third = jnp.stack([-sin_b, cos_b * sin_c, cos_b * cos_c], axis=-1)
    return jnp.stack([first, second, third], axis=1)


def noisy_centres(coords, token_centre_atom, angles, sample_noise_level, centre_noise):
    centre = jnp.take(coords, token_centre_atom, axis=1)
    rotation = rotation_rows(angles)
    turned = rotation[:, :, 0, None] * centre[0][None, None, :]
    turned = turned + rotation[:, :, 1, None] * centre[1][None, None, :]
    turned = turned + rotation[:, :, 2, None] * centre[2][None, None, :]
    return turned + sample_noise_level[:, None, None] * centre_noise


def embed_tokens(single, noisy, sample_noise_level, embedding_weight):
    scaled = noisy / jnp.sqrt(sample_noise_level * sample_noise_level + 1.0)[:, None, None]
    log_level = 0.25 * jnp.log(sample_noise_level)
    hidden_activity = single.astype(jnp.float32)[None] + scaled[:, 0, :, None] * embedding_weight[0]
    hidden_activity = hidden_activity + scaled[:, 1, :, None] * embedding_weight[1]
    hidden_activity = hidden_activity + scaled[:, 2, :, None] * embedding_weight[2]
    hidden_activity = hidden_activity + log_level[:, None, None] * embedding_weight[3]
    return hidden_activity.astype(jnp.bfloat16)


def relay_bias(local_bias):
    blocks, total_heads, row_count, keys_dev = local_bias.shape
    col_count = lax.axis_size("col")
    copies = lax.axis_size("smp")
    group_members = total_heads // col_count
    spread = jnp.broadcast_to(
        local_bias.reshape(blocks, col_count, 1, group_members, row_count, 1, keys_dev),
        (blocks, col_count, copies, group_members, row_count, 1, keys_dev),
    )
    spread = spread.reshape(blocks, col_count * copies * group_members, row_count, 1, keys_dev)
    relayed = lax.all_to_all(spread, ("col", "smp"), split_axis=1, concat_axis=3, tiled=True)
    return relayed.reshape(blocks, group_members, row_count, -1)


def build_absorber(
    query_vectors,
    per_block_bias,
    chain_offset,
    query_chain_labels,
    gathered_chain_ids,
    gathered_key_mask,
    input_scaling,
):
    samples, row_count, group_members, head_size = query_vectors.shape

    def absorb(running, kv_piece, key_start):
        key_count = kv_piece.shape[0]
        key_rows = kv_piece[:, :, 0].reshape(key_count, samples, group_members, head_size)
        value_rows = kv_piece[:, :, 1].reshape(key_count, samples, group_members, head_size)
        attention_logits = (
            jnp.einsum(
                "sqhd,kshd->shqk", query_vectors, key_rows, preferred_element_type=jnp.float32
            )
            * input_scaling
        )
        bias_section = per_block_bias.astype(jnp.float32)
        chain_match = (query_chain_labels[:, None] == gathered_chain_ids[None, :]).astype(
            jnp.float32
        )
        attention_logits = (
            attention_logits
            + bias_section[None]
            + chain_offset[None, :, None, None] * chain_match[None, None]
        )
        attention_logits = jnp.where(
            gathered_key_mask[None, None, None, :] > 0, attention_logits, MASKED
        )
        old_max, old_sum, old_acc = running
        new_max = jnp.maximum(old_max, jnp.max(attention_logits, axis=-1))
        unscaled = jnp.exp(attention_logits - new_max[..., None])
        new_sum = jnp.sum(unscaled, axis=-1)
        new_acc = jnp.einsum(
            "shqk,kshd->shqd",
            unscaled.astype(jnp.bfloat16),
            value_rows,
            preferred_element_type=jnp.float32,
        )
        return (new_max, new_sum, new_acc)

    return absorb


def gather_by_exchange(piece, axis_name, axis):
    count = lax.axis_size(axis_name)
    shape = piece.shape
    spread = jnp.broadcast_to(
        jnp.expand_dims(piece, axis), shape[:axis] + (count,) + shape[axis:]
    )
    joined = lax.all_to_all(spread, axis_name, axis, axis, tiled=True)
    return joined.reshape(shape[:axis] + (count * shape[axis],) + shape[axis + 1 :])


def scatter_sum_rows(partial, axis_name):
    samples, row_count, model_width = partial.shape
    count = lax.axis_size(axis_name)
    pieces = partial.reshape(samples, count, row_count // count, model_width)
    arrived = lax.all_to_all(pieces, axis_name, 1, 1, tiled=True)
    return jnp.sum(arrived.astype(jnp.float32), axis=1)


def body(
    single,
    pair_features,
    coords,
    token_centre_atom,
    chain_label,
    padding_key_mask,
    angles,
    sample_noise_level,
    centre_noise,
    embedding_weight,
    pair_bias_weight,
    same_chain_offset,
    query_key_value_gate_weight,
    attention_output_weight,
    position_update_weight,
):
    noisy = noisy_centres(coords, token_centre_atom, angles, sample_noise_level, centre_noise)
    hidden_activity = embed_tokens(single, noisy, sample_noise_level, embedding_weight)
    pair_normed = layer_norm(pair_features.astype(jnp.float32)).astype(jnp.bfloat16)
    local_bias = jnp.einsum(
        "ikc,cbh->bhik", pair_normed, pair_bias_weight, preferred_element_type=jnp.float32
    ).astype(jnp.bfloat16)
    gathered_pair_bias = relay_bias(local_bias)
    samples, row_count, model_width = hidden_activity.shape
    col_count = lax.axis_size("col")
    own_rows = row_count // col_count
    own_start = lax.axis_index("col") * own_rows
    own_hidden = lax.dynamic_slice_in_dim(hidden_activity, own_start, own_rows, 1)
    normed = layer_norm(hidden_activity.astype(jnp.float32)).astype(jnp.bfloat16)
    group_members = gathered_pair_bias.shape[1]
    head_size = query_key_value_gate_weight.shape[2] // group_members
    group_offset = lax.axis_index("col") * group_members
    input_scaling = head_size ** (-0.5)
    block_count = query_key_value_gate_weight.shape[0]
    for block_index in range(block_count):
        front = jnp.einsum(
            "snd,fed->fsne",
            normed,
            query_key_value_gate_weight[block_index, 0:2],
            preferred_element_type=jnp.float32,
        )
        key_value = jnp.einsum(
            "snd,fed->nsfe",
            normed,
            query_key_value_gate_weight[block_index, 2:4],
            preferred_element_type=jnp.float32,
        ).astype(jnp.bfloat16)
        if block_index == 0:
            key_marks = jnp.stack([chain_label, padding_key_mask], axis=-1).astype(jnp.bfloat16)
            key_marks = jnp.broadcast_to(key_marks[:, None, :, None], (row_count, samples, 2, 1))
            key_marks = jnp.pad(key_marks, ((0, 0), (0, 0), (0, 0), (0, 7)))
            key_value = jnp.concatenate([key_value, key_marks], axis=3)
            key_value, gathered_pair_bias = lax.optimization_barrier(
                (key_value, gathered_pair_bias)
            )
        gathered_key_value = gather_by_exchange(key_value, "row", 0)
        if block_index == 0:
            width = head_size * group_members
            gathered_marks = gathered_key_value[:, 0, :, width].astype(jnp.int32)
            gathered_chain_ids, gathered_key_mask = gathered_marks[:, 0], gathered_marks[:, 1]
            gathered_key_value = gathered_key_value[..., 0:width]
        query_vectors = (
            front[0].astype(jnp.bfloat16).reshape(samples, row_count, group_members, head_size)
        )
        chain_offset = lax.dynamic_slice_in_dim(
            same_chain_offset[block_index], group_offset, group_members, 0
        )
        absorb = build_absorber(
            query_vectors,
            gathered_pair_bias[block_index],
            chain_offset,
            chain_label,
            gathered_chain_ids,
            gathered_key_mask,
            input_scaling,
        )
        start_state = (
            jnp.full((samples, group_members, row_count), LOWEST, jnp.float32),
            jnp.zeros((samples, group_members, row_count), jnp.float32),
            jnp.zeros((samples, group_members, row_count, head_size), jnp.float32),
        )
        final_max, final_sum, final_acc = absorb(
            start_state, gathered_key_value, jnp.int32(0)
        )
        attended = final_acc / final_sum[..., None]
        attended = jnp.transpose(attended, (0, 2, 1, 3)).reshape(
            samples, row_count, group_members * head_size
        )
        gated_output = (jax.nn.sigmoid(front[1]) * attended).astype(jnp.bfloat16)
        partial_out = jnp.einsum(
            "kxp,pj->kxj",
            gated_output,
            attention_output_weight[block_index],
            preferred_element_type=jnp.float32,
        ).astype(jnp.bfloat16)
        summed = scatter_sum_rows(partial_out, "col")
        own_hidden = (own_hidden.astype(jnp.float32) + summed).astype(jnp.bfloat16)
        if block_index + 1 < block_count:
            own_normed = layer_norm(own_hidden.astype(jnp.float32)).astype(jnp.bfloat16)
            normed = gather_by_exchange(own_normed, "col", 1)
    hidden_activity = gather_by_exchange(own_hidden, "col", 1)
    final_normed = layer_norm(hidden_activity.astype(jnp.float32)).astype(jnp.bfloat16)
    update = jnp.einsum(
        "snd,cd->scn", final_normed, position_update_weight, preferred_element_type=jnp.float32
    )
    spread_sq = 1.0 + sample_noise_level * sample_noise_level
    denoised = (
        noisy / spread_sq[:, None, None]
        + (sample_noise_level / jnp.sqrt(spread_sq))[:, None, None] * update
    )
    return (hidden_activity, denoised)


def solution(mesh):
    return jax.shard_map(
        body,
        mesh=mesh,
        in_specs=(
            P("row", None),
            P("row", ("col", "smp"), None),
            P(),
            P("row"),
            P("row"),
            P("row"),
            P("smp", None),
            P("smp"),
            P("smp", None, "row"),
            P(),
            P(),
            P(),
            P(None, None, "col", None),
            P(None, "col", None),
            P(),
        ),
        out_specs=(P("smp", "row", None), P("smp", None, "row")),
        check_vma=False,
    )
```

```python
import jax
import jax.numpy as jnp
from jax import lax
from jax.experimental import pallas as pl
from jax.experimental.pallas import tpu as pltpu
from jax.sharding import PartitionSpec as P

EPSILON = 1e-05
MASKED = -1000000000.0
LOWEST = -1e30


def layer_norm(inputs):
    average = jnp.mean(inputs, axis=-1, keepdims=True)
    centred = inputs - average
    spread = jnp.mean(centred * centred, axis=-1, keepdims=True)
    return centred * lax.rsqrt(spread + EPSILON)


def rotation_rows(angles):
    cos_a = jnp.cos(angles[:, 0])
    sin_a = jnp.sin(angles[:, 0])
    cos_b = jnp.cos(angles[:, 1])
    sin_b = jnp.sin(angles[:, 1])
    cos_c = jnp.cos(angles[:, 2])
    sin_c = jnp.sin(angles[:, 2])
    first = jnp.stack(
        [
            cos_a * cos_b,
            cos_a * sin_b * sin_c - sin_a * cos_c,
            cos_a * sin_b * cos_c + sin_a * sin_c,
        ],
        axis=-1,
    )
    second = jnp.stack(
        [
            sin_a * cos_b,
            sin_a * sin_b * sin_c + cos_a * cos_c,
            sin_a * sin_b * cos_c - cos_a * sin_c,
        ],
        axis=-1,
    )
    third = jnp.stack([-sin_b, cos_b * sin_c, cos_b * cos_c], axis=-1)
    return jnp.stack([first, second, third], axis=1)


def noisy_centres(coords, token_centre_atom, angles, sample_noise_level, centre_noise):
    centre = jnp.take(coords, token_centre_atom, axis=1)
    rotation = rotation_rows(angles)
    turned = rotation[:, :, 0, None] * centre[0][None, None, :]
    turned = turned + rotation[:, :, 1, None] * centre[1][None, None, :]
    turned = turned + rotation[:, :, 2, None] * centre[2][None, None, :]
    return turned + sample_noise_level[:, None, None] * centre_noise


def embed_tokens(single, noisy, sample_noise_level, embedding_weight):
    scaled = noisy / jnp.sqrt(sample_noise_level * sample_noise_level + 1.0)[:, None, None]
    log_level = 0.25 * jnp.log(sample_noise_level)
    hidden_activity = single.astype(jnp.float32)[None] + scaled[:, 0, :, None] * embedding_weight[0]
    hidden_activity = hidden_activity + scaled[:, 1, :, None] * embedding_weight[1]
    hidden_activity = hidden_activity + scaled[:, 2, :, None] * embedding_weight[2]
    hidden_activity = hidden_activity + log_level[:, None, None] * embedding_weight[3]
    return hidden_activity.astype(jnp.bfloat16)


def pair_bias_kernel(pair_ref, weight_ref, out_ref):
    pair = pair_ref[...].astype(jnp.float32)
    average = jnp.mean(pair, axis=-1, keepdims=True)
    centred = pair - average
    spread = jnp.mean(centred * centred, axis=-1, keepdims=True)
    normed = (centred * lax.rsqrt(spread + EPSILON)).astype(jnp.bfloat16)
    out_ref[...] = jnp.dot(normed, weight_ref[...], preferred_element_type=jnp.float32).astype(
        out_ref.dtype
    )


def local_pair_bias(pair_features, pair_bias_weight):
    row_count, keys_dev, channels = pair_features.shape
    _, blocks, total_heads = pair_bias_weight.shape
    pairs = row_count * keys_dev
    outputs = blocks * total_heads
    flat_bias = pl.pallas_call(
        pair_bias_kernel,
        out_shape=jax.ShapeDtypeStruct((pairs, outputs), jnp.bfloat16),
        in_specs=[pl.BlockSpec(memory_space=pltpu.VMEM)] * 2,
        out_specs=pl.BlockSpec(memory_space=pltpu.VMEM),
        cost_estimate=pl.CostEstimate(
            flops=2 * pairs * channels * outputs + 8 * pairs * channels,
            transcendentals=pairs,
            bytes_accessed=2 * (pairs * channels + channels * outputs + pairs * outputs),
        ),
    )(pair_features.reshape(pairs, channels), pair_bias_weight.reshape(channels, outputs))
    flat_bias = flat_bias.reshape(row_count, keys_dev, blocks, total_heads)
    return jnp.transpose(flat_bias, (2, 3, 0, 1))


def relay_bias(local_bias):
    blocks, total_heads, row_count, keys_dev = local_bias.shape
    col_count = lax.axis_size("col")
    copies = lax.axis_size("smp")
    group_members = total_heads // col_count
    spread = jnp.broadcast_to(
        local_bias.reshape(blocks, col_count, 1, group_members, row_count, 1, keys_dev),
        (blocks, col_count, copies, group_members, row_count, 1, keys_dev),
    )
    spread = spread.reshape(blocks, col_count * copies * group_members, row_count, 1, keys_dev)
    relayed = lax.all_to_all(spread, ("col", "smp"), split_axis=1, concat_axis=3, tiled=True)
    return relayed.reshape(blocks, group_members, row_count, -1)


def build_absorber(
    query_vectors,
    per_block_bias,
    chain_offset,
    query_chain_labels,
    gathered_chain_ids,
    gathered_key_mask,
    input_scaling,
):
    samples, row_count, group_members, head_size = query_vectors.shape

    def absorb(running, kv_piece, key_start):
        key_count = kv_piece.shape[0]
        key_rows = kv_piece[:, :, 0].reshape(key_count, samples, group_members, head_size)
        value_rows = kv_piece[:, :, 1].reshape(key_count, samples, group_members, head_size)
        attention_logits = (
            jnp.einsum(
                "sqhd,kshd->shqk", query_vectors, key_rows, preferred_element_type=jnp.float32
            )
            * input_scaling
        )
        bias_section = per_block_bias.astype(jnp.float32)
        chain_match = (query_chain_labels[:, None] == gathered_chain_ids[None, :]).astype(
            jnp.float32
        )
        attention_logits = (
            attention_logits
            + bias_section[None]
            + chain_offset[None, :, None, None] * chain_match[None, None]
        )
        attention_logits = jnp.where(
            gathered_key_mask[None, None, None, :] > 0, attention_logits, MASKED
        )
        old_max, old_sum, old_acc = running
        new_max = jnp.maximum(old_max, jnp.max(attention_logits, axis=-1))
        unscaled = jnp.exp(attention_logits - new_max[..., None])
        new_sum = jnp.sum(unscaled, axis=-1)
        new_acc = jnp.einsum(
            "shqk,kshd->shqd",
            unscaled.astype(jnp.bfloat16),
            value_rows,
            preferred_element_type=jnp.float32,
        )
        return (new_max, new_sum, new_acc)

    return absorb


def gather_by_exchange(piece, axis_name, axis):
    count = lax.axis_size(axis_name)
    shape = piece.shape
    spread = jnp.broadcast_to(
        jnp.expand_dims(piece, axis), shape[:axis] + (count,) + shape[axis:]
    )
    joined = lax.all_to_all(spread, axis_name, axis, axis, tiled=True)
    return joined.reshape(shape[:axis] + (count * shape[axis],) + shape[axis + 1 :])


def scatter_sum_rows(partial, axis_name):
    samples, row_count, model_width = partial.shape
    count = lax.axis_size(axis_name)
    pieces = partial.reshape(samples, count, row_count // count, model_width)
    arrived = lax.all_to_all(pieces, axis_name, 1, 1, tiled=True)
    return jnp.sum(arrived.astype(jnp.float32), axis=1)


def body(
    single,
    pair_features,
    coords,
    token_centre_atom,
    chain_label,
    padding_key_mask,
    angles,
    sample_noise_level,
    centre_noise,
    embedding_weight,
    pair_bias_weight,
    same_chain_offset,
    query_key_value_gate_weight,
    attention_output_weight,
    position_update_weight,
):
    noisy = noisy_centres(coords, token_centre_atom, angles, sample_noise_level, centre_noise)
    hidden_activity = embed_tokens(single, noisy, sample_noise_level, embedding_weight)
    local_bias = local_pair_bias(pair_features, pair_bias_weight)
    gathered_pair_bias = relay_bias(local_bias)
    samples, row_count, model_width = hidden_activity.shape
    col_count = lax.axis_size("col")
    own_rows = row_count // col_count
    own_start = lax.axis_index("col") * own_rows
    own_hidden = lax.dynamic_slice_in_dim(hidden_activity, own_start, own_rows, 1)
    normed = layer_norm(hidden_activity.astype(jnp.float32)).astype(jnp.bfloat16)
    group_members = gathered_pair_bias.shape[1]
    head_size = query_key_value_gate_weight.shape[2] // group_members
    group_offset = lax.axis_index("col") * group_members
    input_scaling = head_size ** (-0.5)
    block_count = query_key_value_gate_weight.shape[0]
    for block_index in range(block_count):
        front = jnp.einsum(
            "snd,fed->fsne",
            normed,
            query_key_value_gate_weight[block_index, 0:2],
            preferred_element_type=jnp.float32,
        )
        key_value = jnp.einsum(
            "snd,fed->nsfe",
            normed,
            query_key_value_gate_weight[block_index, 2:4],
            preferred_element_type=jnp.float32,
        ).astype(jnp.bfloat16)
        if block_index == 0:
            key_marks = jnp.stack([chain_label, padding_key_mask], axis=-1).astype(jnp.bfloat16)
            key_marks = jnp.broadcast_to(key_marks[:, None, :, None], (row_count, samples, 2, 1))
            key_marks = jnp.pad(key_marks, ((0, 0), (0, 0), (0, 0), (0, 7)))
            key_value = jnp.concatenate([key_value, key_marks], axis=3)
            key_value, gathered_pair_bias = lax.optimization_barrier(
                (key_value, gathered_pair_bias)
            )
        gathered_key_value = gather_by_exchange(key_value, "row", 0)
        if block_index == 0:
            width = head_size * group_members
            gathered_marks = gathered_key_value[:, 0, :, width].astype(jnp.int32)
            gathered_chain_ids, gathered_key_mask = gathered_marks[:, 0], gathered_marks[:, 1]
            gathered_key_value = gathered_key_value[..., 0:width]
        query_vectors = (
            front[0].astype(jnp.bfloat16).reshape(samples, row_count, group_members, head_size)
        )
        chain_offset = lax.dynamic_slice_in_dim(
            same_chain_offset[block_index], group_offset, group_members, 0
        )
        absorb = build_absorber(
            query_vectors,
            gathered_pair_bias[block_index],
            chain_offset,
            chain_label,
            gathered_chain_ids,
            gathered_key_mask,
            input_scaling,
        )
        start_state = (
            jnp.full((samples, group_members, row_count), LOWEST, jnp.float32),
            jnp.zeros((samples, group_members, row_count), jnp.float32),
            jnp.zeros((samples, group_members, row_count, head_size), jnp.float32),
        )
        final_max, final_sum, final_acc = absorb(
            start_state, gathered_key_value, jnp.int32(0)
        )
        attended = final_acc / final_sum[..., None]
        attended = jnp.transpose(attended, (0, 2, 1, 3)).reshape(
            samples, row_count, group_members * head_size
        )
        gated_output = (jax.nn.sigmoid(front[1]) * attended).astype(jnp.bfloat16)
        partial_out = jnp.einsum(
            "kxp,pj->kxj",
            gated_output,
            attention_output_weight[block_index],
            preferred_element_type=jnp.float32,
        ).astype(jnp.bfloat16)
        summed = scatter_sum_rows(partial_out, "col")
        own_hidden = (own_hidden.astype(jnp.float32) + summed).astype(jnp.bfloat16)
        if block_index + 1 < block_count:
            own_normed = layer_norm(own_hidden.astype(jnp.float32)).astype(jnp.bfloat16)
            normed = gather_by_exchange(own_normed, "col", 1)
    hidden_activity = gather_by_exchange(own_hidden, "col", 1)
    final_normed = layer_norm(hidden_activity.astype(jnp.float32)).astype(jnp.bfloat16)
    update = jnp.einsum(
        "snd,cd->scn", final_normed, position_update_weight, preferred_element_type=jnp.float32
    )
    spread_sq = 1.0 + sample_noise_level * sample_noise_level
    denoised = (
        noisy / spread_sq[:, None, None]
        + (sample_noise_level / jnp.sqrt(spread_sq))[:, None, None] * update
    )
    return (hidden_activity, denoised)


def solution(mesh):
    return jax.shard_map(
        body,
        mesh=mesh,
        in_specs=(
            P("row", None),
            P("row", ("col", "smp"), None),
            P(),
            P("row"),
            P("row"),
            P("row"),
            P("smp", None),
            P("smp"),
            P("smp", None, "row"),
            P(),
            P(),
            P(),
            P(None, None, "col", None),
            P(None, "col", None),
            P(),
        ),
        out_specs=(P("smp", "row", None), P("smp", None, "row")),
        check_vma=False,
    )
```

```python
import jax
import jax.numpy as jnp
from jax import lax
from jax.sharding import PartitionSpec as P

EPSILON = 1e-05
MASKED = -1000000000.0
LOWEST = -1e30


def layer_norm(inputs):
    average = jnp.mean(inputs, axis=-1, keepdims=True)
    centred = inputs - average
    spread = jnp.mean(centred * centred, axis=-1, keepdims=True)
    return centred * lax.rsqrt(spread + EPSILON)


def rotation_rows(angles):
    cos_a = jnp.cos(angles[:, 0])
    sin_a = jnp.sin(angles[:, 0])
    cos_b = jnp.cos(angles[:, 1])
    sin_b = jnp.sin(angles[:, 1])
    cos_c = jnp.cos(angles[:, 2])
    sin_c = jnp.sin(angles[:, 2])
    first = jnp.stack(
        [
            cos_a * cos_b,
            cos_a * sin_b * sin_c - sin_a * cos_c,
            cos_a * sin_b * cos_c + sin_a * sin_c,
        ],
        axis=-1,
    )
    second = jnp.stack(
        [
            sin_a * cos_b,
            sin_a * sin_b * sin_c + cos_a * cos_c,
            sin_a * sin_b * cos_c - cos_a * sin_c,
        ],
        axis=-1,
    )
    third = jnp.stack([-sin_b, cos_b * sin_c, cos_b * cos_c], axis=-1)
    return jnp.stack([first, second, third], axis=1)


def noisy_centres(coords, token_centre_atom, angles, sample_noise_level, centre_noise):
    centre = jnp.take(coords, token_centre_atom, axis=1)
    rotation = rotation_rows(angles)
    turned = rotation[:, :, 0, None] * centre[0][None, None, :]
    turned = turned + rotation[:, :, 1, None] * centre[1][None, None, :]
    turned = turned + rotation[:, :, 2, None] * centre[2][None, None, :]
    return turned + sample_noise_level[:, None, None] * centre_noise


def embed_tokens(single, noisy, sample_noise_level, embedding_weight):
    scaled = noisy / jnp.sqrt(sample_noise_level * sample_noise_level + 1.0)[:, None, None]
    log_level = 0.25 * jnp.log(sample_noise_level)
    hidden_activity = single.astype(jnp.float32)[None] + scaled[:, 0, :, None] * embedding_weight[0]
    hidden_activity = hidden_activity + scaled[:, 1, :, None] * embedding_weight[1]
    hidden_activity = hidden_activity + scaled[:, 2, :, None] * embedding_weight[2]
    hidden_activity = hidden_activity + log_level[:, None, None] * embedding_weight[3]
    return hidden_activity.astype(jnp.bfloat16)


def relay_bias(local_bias):
    blocks, total_heads, row_count, keys_dev = local_bias.shape
    col_count = lax.axis_size("col")
    group_members = total_heads // col_count
    by_group = local_bias.reshape(blocks, col_count, group_members, row_count, 1, keys_dev)
    return lax.all_to_all(by_group, "col", 1, 4, tiled=True)


def spread_bias(column_bias):
    blocks, _, group_members, row_count, col_count, keys_dev = column_bias.shape
    copies = lax.axis_size("smp")
    forward = [(i, (i + 1) % copies) for i in range(copies)]
    backward = [(i, (i - 1) % copies) for i in range(copies)]
    pieces = {0: column_bias}
    rightward, leftward = column_bias, column_bias
    for step in range(1, copies // 2 + 1):
        rightward = lax.ppermute(rightward, "smp", forward)
        pieces[-step] = rightward
        if step < copies - copies // 2:
            leftward = lax.ppermute(leftward, "smp", backward)
            pieces[step] = leftward
    offsets = sorted(pieces)
    stacked = jnp.concatenate([pieces[d] for d in offsets], axis=1)
    stacked = jnp.roll(stacked, lax.axis_index("smp") + offsets[0], axis=1)
    stacked = jnp.transpose(stacked, (0, 2, 3, 4, 1, 5))
    return stacked.reshape(blocks, group_members, row_count, col_count * copies * keys_dev)


def build_absorber(
    query_vectors,
    per_block_bias,
    chain_offset,
    query_chain_labels,
    gathered_chain_ids,
    gathered_key_mask,
    input_scaling,
):
    samples, row_count, group_members, head_size = query_vectors.shape

    def absorb(running, kv_piece, key_start):
        key_count = kv_piece.shape[0]
        key_rows = kv_piece[:, :, 0].reshape(key_count, samples, group_members, head_size)
        value_rows = kv_piece[:, :, 1].reshape(key_count, samples, group_members, head_size)
        attention_logits = (
            jnp.einsum(
                "sqhd,kshd->shqk", query_vectors, key_rows, preferred_element_type=jnp.float32
            )
            * input_scaling
        )
        bias_section = per_block_bias.astype(jnp.float32)
        chain_match = (query_chain_labels[:, None] == gathered_chain_ids[None, :]).astype(
            jnp.float32
        )
        attention_logits = (
            attention_logits
            + bias_section[None]
            + chain_offset[None, :, None, None] * chain_match[None, None]
        )
        attention_logits = jnp.where(
            gathered_key_mask[None, None, None, :] > 0, attention_logits, MASKED
        )
        old_max, old_sum, old_acc = running
        new_max = jnp.maximum(old_max, jnp.max(attention_logits, axis=-1))
        unscaled = jnp.exp(attention_logits - new_max[..., None])
        new_sum = jnp.sum(unscaled, axis=-1)
        new_acc = jnp.einsum(
            "shqk,kshd->shqd",
            unscaled.astype(jnp.bfloat16),
            value_rows,
            preferred_element_type=jnp.float32,
        )
        return (new_max, new_sum, new_acc)

    return absorb


def gather_by_exchange(piece, axis_name, axis):
    count = lax.axis_size(axis_name)
    shape = piece.shape
    spread = jnp.broadcast_to(
        jnp.expand_dims(piece, axis), shape[:axis] + (count,) + shape[axis:]
    )
    joined = lax.all_to_all(spread, axis_name, axis, axis, tiled=True)
    return joined.reshape(shape[:axis] + (count * shape[axis],) + shape[axis + 1 :])


def scatter_sum_rows(partial, axis_name):
    samples, row_count, model_width = partial.shape
    count = lax.axis_size(axis_name)
    pieces = partial.reshape(samples, count, row_count // count, model_width)
    arrived = lax.all_to_all(pieces, axis_name, 1, 1, tiled=True)
    return jnp.sum(arrived.astype(jnp.float32), axis=1)


def body(
    single,
    pair_features,
    coords,
    token_centre_atom,
    chain_label,
    padding_key_mask,
    angles,
    sample_noise_level,
    centre_noise,
    embedding_weight,
    pair_bias_weight,
    same_chain_offset,
    query_key_value_gate_weight,
    attention_output_weight,
    position_update_weight,
):
    noisy = noisy_centres(coords, token_centre_atom, angles, sample_noise_level, centre_noise)
    hidden_activity = embed_tokens(single, noisy, sample_noise_level, embedding_weight)
    pair_normed = layer_norm(pair_features.astype(jnp.float32)).astype(jnp.bfloat16)
    local_bias = jnp.einsum(
        "ikc,cbh->bhik", pair_normed, pair_bias_weight, preferred_element_type=jnp.float32
    ).astype(jnp.bfloat16)
    column_bias = relay_bias(local_bias)
    gathered_pair_bias = spread_bias(column_bias)
    samples, row_count, model_width = hidden_activity.shape
    col_count = lax.axis_size("col")
    own_rows = row_count // col_count
    own_start = lax.axis_index("col") * own_rows
    own_hidden = lax.dynamic_slice_in_dim(hidden_activity, own_start, own_rows, 1)
    normed = layer_norm(hidden_activity.astype(jnp.float32)).astype(jnp.bfloat16)
    group_members = gathered_pair_bias.shape[1]
    head_size = query_key_value_gate_weight.shape[2] // group_members
    group_offset = lax.axis_index("col") * group_members
    input_scaling = head_size ** (-0.5)
    block_count = query_key_value_gate_weight.shape[0]
    for block_index in range(block_count):
        front = jnp.einsum(
            "snd,fed->fsne",
            normed,
            query_key_value_gate_weight[block_index, 0:2],
            preferred_element_type=jnp.float32,
        )
        key_value = jnp.einsum(
            "snd,fed->nsfe",
            normed,
            query_key_value_gate_weight[block_index, 2:4],
            preferred_element_type=jnp.float32,
        ).astype(jnp.bfloat16)
        if block_index == 0:
            key_marks = jnp.stack([chain_label, padding_key_mask], axis=-1).astype(jnp.bfloat16)
            key_marks = jnp.broadcast_to(key_marks[:, None, :, None], (row_count, samples, 2, 1))
            key_marks = jnp.pad(key_marks, ((0, 0), (0, 0), (0, 0), (0, 7)))
            key_value = jnp.concatenate([key_value, key_marks], axis=3)
            key_value, _ = lax.optimization_barrier((key_value, column_bias))
        gathered_key_value = gather_by_exchange(key_value, "row", 0)
        if block_index == 0:
            width = head_size * group_members
            gathered_marks = gathered_key_value[:, 0, :, width].astype(jnp.int32)
            gathered_chain_ids, gathered_key_mask = gathered_marks[:, 0], gathered_marks[:, 1]
            gathered_key_value = gathered_key_value[..., 0:width]
        query_vectors = (
            front[0].astype(jnp.bfloat16).reshape(samples, row_count, group_members, head_size)
        )
        chain_offset = lax.dynamic_slice_in_dim(
            same_chain_offset[block_index], group_offset, group_members, 0
        )
        absorb = build_absorber(
            query_vectors,
            gathered_pair_bias[block_index],
            chain_offset,
            chain_label,
            gathered_chain_ids,
            gathered_key_mask,
            input_scaling,
        )
        start_state = (
            jnp.full((samples, group_members, row_count), LOWEST, jnp.float32),
            jnp.zeros((samples, group_members, row_count), jnp.float32),
            jnp.zeros((samples, group_members, row_count, head_size), jnp.float32),
        )
        final_max, final_sum, final_acc = absorb(
            start_state, gathered_key_value, jnp.int32(0)
        )
        attended = final_acc / final_sum[..., None]
        attended = jnp.transpose(attended, (0, 2, 1, 3)).reshape(
            samples, row_count, group_members * head_size
        )
        gated_output = (jax.nn.sigmoid(front[1]) * attended).astype(jnp.bfloat16)
        partial_out = jnp.einsum(
            "kxp,pj->kxj",
            gated_output,
            attention_output_weight[block_index],
            preferred_element_type=jnp.float32,
        ).astype(jnp.bfloat16)
        summed = scatter_sum_rows(partial_out, "col")
        own_hidden = (own_hidden.astype(jnp.float32) + summed).astype(jnp.bfloat16)
        if block_index + 1 < block_count:
            own_normed = layer_norm(own_hidden.astype(jnp.float32)).astype(jnp.bfloat16)
            normed = gather_by_exchange(own_normed, "col", 1)
    hidden_activity = gather_by_exchange(own_hidden, "col", 1)
    final_normed = layer_norm(hidden_activity.astype(jnp.float32)).astype(jnp.bfloat16)
    update = jnp.einsum(
        "snd,cd->scn", final_normed, position_update_weight, preferred_element_type=jnp.float32
    )
    spread_sq = 1.0 + sample_noise_level * sample_noise_level
    denoised = (
        noisy / spread_sq[:, None, None]
        + (sample_noise_level / jnp.sqrt(spread_sq))[:, None, None] * update
    )
    return (hidden_activity, denoised)


def solution(mesh):
    return jax.shard_map(
        body,
        mesh=mesh,
        in_specs=(
            P("row", None),
            P("row", ("col", "smp"), None),
            P(),
            P("row"),
            P("row"),
            P("row"),
            P("smp", None),
            P("smp"),
            P("smp", None, "row"),
            P(),
            P(),
            P(),
            P(None, None, "col", None),
            P(None, "col", None),
            P(),
        ),
        out_specs=(P("smp", "row", None), P("smp", None, "row")),
        check_vma=False,
    )
```

```python
import jax
import jax.numpy as jnp
from jax import lax
from jax.sharding import PartitionSpec as P

EPSILON = 1e-05
MASKED = -1000000000.0
LOWEST = -1e30


def layer_norm(inputs):
    average = jnp.mean(inputs, axis=-1, keepdims=True)
    centred = inputs - average
    spread = jnp.mean(centred * centred, axis=-1, keepdims=True)
    return centred * lax.rsqrt(spread + EPSILON)


def rotation_rows(angles):
    cos_a = jnp.cos(angles[:, 0])
    sin_a = jnp.sin(angles[:, 0])
    cos_b = jnp.cos(angles[:, 1])
    sin_b = jnp.sin(angles[:, 1])
    cos_c = jnp.cos(angles[:, 2])
    sin_c = jnp.sin(angles[:, 2])
    first = jnp.stack(
        [
            cos_a * cos_b,
            cos_a * sin_b * sin_c - sin_a * cos_c,
            cos_a * sin_b * cos_c + sin_a * sin_c,
        ],
        axis=-1,
    )
    second = jnp.stack(
        [
            sin_a * cos_b,
            sin_a * sin_b * sin_c + cos_a * cos_c,
            sin_a * sin_b * cos_c - cos_a * sin_c,
        ],
        axis=-1,
    )
    third = jnp.stack([-sin_b, cos_b * sin_c, cos_b * cos_c], axis=-1)
    return jnp.stack([first, second, third], axis=1)


def noisy_centres(coords, token_centre_atom, angles, sample_noise_level, centre_noise):
    centre = jnp.take(coords, token_centre_atom, axis=1)
    rotation = rotation_rows(angles)
    turned = rotation[:, :, 0, None] * centre[0][None, None, :]
    turned = turned + rotation[:, :, 1, None] * centre[1][None, None, :]
    turned = turned + rotation[:, :, 2, None] * centre[2][None, None, :]
    return turned + sample_noise_level[:, None, None] * centre_noise


def embed_tokens(single, noisy, sample_noise_level, embedding_weight):
    scaled = noisy / jnp.sqrt(sample_noise_level * sample_noise_level + 1.0)[:, None, None]
    log_level = 0.25 * jnp.log(sample_noise_level)
    hidden_activity = single.astype(jnp.float32)[None] + scaled[:, 0, :, None] * embedding_weight[0]
    hidden_activity = hidden_activity + scaled[:, 1, :, None] * embedding_weight[1]
    hidden_activity = hidden_activity + scaled[:, 2, :, None] * embedding_weight[2]
    hidden_activity = hidden_activity + log_level[:, None, None] * embedding_weight[3]
    return hidden_activity.astype(jnp.bfloat16)


def relay_bias(local_bias):
    blocks, total_heads, row_count, keys_dev = local_bias.shape
    col_count = lax.axis_size("col")
    group_members = total_heads // col_count
    by_group = local_bias.reshape(blocks, col_count, group_members, row_count, 1, keys_dev)
    return lax.all_to_all(by_group, "col", 1, 4, tiled=True)


def spread_bias(column_bias):
    blocks, _, group_members, row_count, col_count, keys_dev = column_bias.shape
    copies = lax.axis_size("smp")
    forward = [(i, (i + 1) % copies) for i in range(copies)]
    backward = [(i, (i - 1) % copies) for i in range(copies)]
    pieces = {0: column_bias}
    rightward, leftward = column_bias, column_bias
    for step in range(1, copies // 2 + 1):
        rightward = lax.ppermute(rightward, "smp", forward)
        pieces[-step] = rightward
        if step < copies - copies // 2:
            leftward = lax.ppermute(leftward, "smp", backward)
            pieces[step] = leftward
    offsets = sorted(pieces)
    stacked = jnp.concatenate([pieces[d] for d in offsets], axis=1)
    stacked = jnp.roll(stacked, lax.axis_index("smp") + offsets[0], axis=1)
    stacked = jnp.transpose(stacked, (0, 2, 3, 4, 1, 5))
    return stacked.reshape(blocks, group_members, row_count, col_count * copies * keys_dev)


def build_absorber(
    query_vectors,
    per_block_bias,
    chain_offset,
    query_chain_labels,
    gathered_chain_ids,
    gathered_key_mask,
    input_scaling,
):
    samples, row_count, group_members, head_size = query_vectors.shape

    def absorb(running, kv_piece, key_start):
        key_count = kv_piece.shape[0]
        key_rows = kv_piece[:, :, 0].reshape(key_count, samples, group_members, head_size)
        value_rows = kv_piece[:, :, 1].reshape(key_count, samples, group_members, head_size)
        attention_logits = (
            jnp.einsum(
                "sqhd,kshd->shqk", query_vectors, key_rows, preferred_element_type=jnp.float32
            )
            * input_scaling
        )
        bias_section = per_block_bias.astype(jnp.float32)
        chain_match = (query_chain_labels[:, None] == gathered_chain_ids[None, :]).astype(
            jnp.float32
        )
        attention_logits = (
            attention_logits
            + bias_section[None]
            + chain_offset[None, :, None, None] * chain_match[None, None]
        )
        attention_logits = jnp.where(
            gathered_key_mask[None, None, None, :] > 0, attention_logits, MASKED
        )
        old_max, old_sum, old_acc = running
        new_max = jnp.maximum(old_max, jnp.max(attention_logits, axis=-1))
        unscaled = jnp.exp(attention_logits - new_max[..., None])
        new_sum = jnp.sum(unscaled, axis=-1)
        new_acc = jnp.einsum(
            "shqk,kshd->shqd",
            unscaled.astype(jnp.bfloat16),
            value_rows,
            preferred_element_type=jnp.float32,
        )
        return (new_max, new_sum, new_acc)

    return absorb


def gather_by_exchange(piece, axis_name, axis):
    count = lax.axis_size(axis_name)
    shape = piece.shape
    spread = jnp.broadcast_to(
        jnp.expand_dims(piece, axis), shape[:axis] + (count,) + shape[axis:]
    )
    joined = lax.all_to_all(spread, axis_name, axis, axis, tiled=True)
    return joined.reshape(shape[:axis] + (count * shape[axis],) + shape[axis + 1 :])


def scatter_sum_rows(partial, axis_name):
    samples, row_count, model_width = partial.shape
    count = lax.axis_size(axis_name)
    pieces = partial.reshape(samples, count, row_count // count, model_width)
    arrived = lax.all_to_all(pieces, axis_name, 1, 1, tiled=True)
    return jnp.sum(arrived.astype(jnp.float32), axis=1)


def body(
    single,
    pair_features,
    coords,
    token_centre_atom,
    chain_label,
    padding_key_mask,
    angles,
    sample_noise_level,
    centre_noise,
    embedding_weight,
    pair_bias_weight,
    same_chain_offset,
    query_key_value_gate_weight,
    attention_output_weight,
    position_update_weight,
):
    noisy = noisy_centres(coords, token_centre_atom, angles, sample_noise_level, centre_noise)
    hidden_activity = embed_tokens(single, noisy, sample_noise_level, embedding_weight)
    pair_normed = layer_norm(pair_features.astype(jnp.float32)).astype(jnp.bfloat16)
    local_bias = jnp.einsum(
        "ikc,cbh->bhik", pair_normed, pair_bias_weight, preferred_element_type=jnp.float32
    ).astype(jnp.bfloat16)
    column_bias = relay_bias(local_bias)
    first_bias = spread_bias(column_bias[:1])
    later_bias = spread_bias(column_bias[1:])
    samples, row_count, model_width = hidden_activity.shape
    col_count = lax.axis_size("col")
    own_rows = row_count // col_count
    own_start = lax.axis_index("col") * own_rows
    own_hidden = lax.dynamic_slice_in_dim(hidden_activity, own_start, own_rows, 1)
    normed = layer_norm(hidden_activity.astype(jnp.float32)).astype(jnp.bfloat16)
    group_members = first_bias.shape[1]
    head_size = query_key_value_gate_weight.shape[2] // group_members
    group_offset = lax.axis_index("col") * group_members
    input_scaling = head_size ** (-0.5)
    block_count = query_key_value_gate_weight.shape[0]
    for block_index in range(block_count):
        front = jnp.einsum(
            "snd,fed->fsne",
            normed,
            query_key_value_gate_weight[block_index, 0:2],
            preferred_element_type=jnp.float32,
        )
        key_value = jnp.einsum(
            "snd,fed->nsfe",
            normed,
            query_key_value_gate_weight[block_index, 2:4],
            preferred_element_type=jnp.float32,
        ).astype(jnp.bfloat16)
        if block_index == 0:
            key_marks = jnp.stack([chain_label, padding_key_mask], axis=-1).astype(jnp.bfloat16)
            key_marks = jnp.broadcast_to(key_marks[:, None, :, None], (row_count, samples, 2, 1))
            key_marks = jnp.pad(key_marks, ((0, 0), (0, 0), (0, 0), (0, 7)))
            key_value = jnp.concatenate([key_value, key_marks], axis=3)
            key_value, _ = lax.optimization_barrier((key_value, column_bias))
        gathered_key_value = gather_by_exchange(key_value, "row", 0)
        if block_index == 0:
            width = head_size * group_members
            gathered_marks = gathered_key_value[:, 0, :, width].astype(jnp.int32)
            gathered_chain_ids, gathered_key_mask = gathered_marks[:, 0], gathered_marks[:, 1]
            gathered_key_value = gathered_key_value[..., 0:width]
        query_vectors = (
            front[0].astype(jnp.bfloat16).reshape(samples, row_count, group_members, head_size)
        )
        chain_offset = lax.dynamic_slice_in_dim(
            same_chain_offset[block_index], group_offset, group_members, 0
        )
        absorb = build_absorber(
            query_vectors,
            first_bias[0] if block_index == 0 else later_bias[block_index - 1],
            chain_offset,
            chain_label,
            gathered_chain_ids,
            gathered_key_mask,
            input_scaling,
        )
        start_state = (
            jnp.full((samples, group_members, row_count), LOWEST, jnp.float32),
            jnp.zeros((samples, group_members, row_count), jnp.float32),
            jnp.zeros((samples, group_members, row_count, head_size), jnp.float32),
        )
        final_max, final_sum, final_acc = absorb(
            start_state, gathered_key_value, jnp.int32(0)
        )
        attended = final_acc / final_sum[..., None]
        attended = jnp.transpose(attended, (0, 2, 1, 3)).reshape(
            samples, row_count, group_members * head_size
        )
        gated_output = (jax.nn.sigmoid(front[1]) * attended).astype(jnp.bfloat16)
        partial_out = jnp.einsum(
            "kxp,pj->kxj",
            gated_output,
            attention_output_weight[block_index],
            preferred_element_type=jnp.float32,
        ).astype(jnp.bfloat16)
        summed = scatter_sum_rows(partial_out, "col")
        own_hidden = (own_hidden.astype(jnp.float32) + summed).astype(jnp.bfloat16)
        if block_index + 1 < block_count:
            own_normed = layer_norm(own_hidden.astype(jnp.float32)).astype(jnp.bfloat16)
            normed = gather_by_exchange(own_normed, "col", 1)
    hidden_activity = gather_by_exchange(own_hidden, "col", 1)
    final_normed = layer_norm(hidden_activity.astype(jnp.float32)).astype(jnp.bfloat16)
    update = jnp.einsum(
        "snd,cd->scn", final_normed, position_update_weight, preferred_element_type=jnp.float32
    )
    spread_sq = 1.0 + sample_noise_level * sample_noise_level
    denoised = (
        noisy / spread_sq[:, None, None]
        + (sample_noise_level / jnp.sqrt(spread_sq))[:, None, None] * update
    )
    return (hidden_activity, denoised)


def solution(mesh):
    return jax.shard_map(
        body,
        mesh=mesh,
        in_specs=(
            P("row", None),
            P("row", ("col", "smp"), None),
            P(),
            P("row"),
            P("row"),
            P("row"),
            P("smp", None),
            P("smp"),
            P("smp", None, "row"),
            P(),
            P(),
            P(),
            P(None, None, "col", None),
            P(None, "col", None),
            P(),
        ),
        out_specs=(P("smp", "row", None), P("smp", None, "row")),
        check_vma=False,
    )
```

```python
import jax
import jax.numpy as jnp
from jax import lax
from jax.sharding import PartitionSpec as P

EPSILON = 1e-05
MASKED = -1000000000.0
LOWEST = -1e30


def layer_norm(inputs):
    average = jnp.mean(inputs, axis=-1, keepdims=True)
    centred = inputs - average
    spread = jnp.mean(centred * centred, axis=-1, keepdims=True)
    return centred * lax.rsqrt(spread + EPSILON)


def rotation_rows(angles):
    cos_a = jnp.cos(angles[:, 0])
    sin_a = jnp.sin(angles[:, 0])
    cos_b = jnp.cos(angles[:, 1])
    sin_b = jnp.sin(angles[:, 1])
    cos_c = jnp.cos(angles[:, 2])
    sin_c = jnp.sin(angles[:, 2])
    first = jnp.stack(
        [
            cos_a * cos_b,
            cos_a * sin_b * sin_c - sin_a * cos_c,
            cos_a * sin_b * cos_c + sin_a * sin_c,
        ],
        axis=-1,
    )
    second = jnp.stack(
        [
            sin_a * cos_b,
            sin_a * sin_b * sin_c + cos_a * cos_c,
            sin_a * sin_b * cos_c - cos_a * sin_c,
        ],
        axis=-1,
    )
    third = jnp.stack([-sin_b, cos_b * sin_c, cos_b * cos_c], axis=-1)
    return jnp.stack([first, second, third], axis=1)


def noisy_centres(coords, token_centre_atom, angles, sample_noise_level, centre_noise):
    centre = jnp.take(coords, token_centre_atom, axis=1)
    rotation = rotation_rows(angles)
    turned = rotation[:, :, 0, None] * centre[0][None, None, :]
    turned = turned + rotation[:, :, 1, None] * centre[1][None, None, :]
    turned = turned + rotation[:, :, 2, None] * centre[2][None, None, :]
    return turned + sample_noise_level[:, None, None] * centre_noise


def embed_tokens(single, noisy, sample_noise_level, embedding_weight):
    scaled = noisy / jnp.sqrt(sample_noise_level * sample_noise_level + 1.0)[:, None, None]
    log_level = 0.25 * jnp.log(sample_noise_level)
    hidden_activity = single.astype(jnp.float32)[None] + scaled[:, 0, :, None] * embedding_weight[0]
    hidden_activity = hidden_activity + scaled[:, 1, :, None] * embedding_weight[1]
    hidden_activity = hidden_activity + scaled[:, 2, :, None] * embedding_weight[2]
    hidden_activity = hidden_activity + log_level[:, None, None] * embedding_weight[3]
    return hidden_activity.astype(jnp.bfloat16)


def relay_bias(local_bias):
    blocks, total_heads, row_count, keys_dev = local_bias.shape
    col_count = lax.axis_size("col")
    group_members = total_heads // col_count
    by_group = local_bias.reshape(blocks, col_count, group_members, row_count, 1, keys_dev)
    return lax.all_to_all(by_group, "col", 1, 4, tiled=True)


def spread_bias(column_bias):
    blocks, _, group_members, row_count, col_count, keys_dev = column_bias.shape
    copies = lax.axis_size("smp")
    forward = [(i, (i + 1) % copies) for i in range(copies)]
    backward = [(i, (i - 1) % copies) for i in range(copies)]
    pieces = {0: column_bias}
    rightward, leftward = column_bias, column_bias
    first_hop = None
    for step in range(1, copies // 2 + 1):
        rightward = lax.ppermute(rightward, "smp", forward)
        pieces[-step] = rightward
        if step < copies - copies // 2:
            leftward = lax.ppermute(leftward, "smp", backward)
            pieces[step] = leftward
        if first_hop is None:
            first_hop = (rightward, leftward)
    offsets = sorted(pieces)
    stacked = jnp.concatenate([pieces[d] for d in offsets], axis=1)
    stacked = jnp.roll(stacked, lax.axis_index("smp") + offsets[0], axis=1)
    stacked = jnp.transpose(stacked, (0, 2, 3, 4, 1, 5))
    spread = stacked.reshape(blocks, group_members, row_count, col_count * copies * keys_dev)
    return spread, first_hop


def build_absorber(
    query_vectors,
    per_block_bias,
    chain_offset,
    query_chain_labels,
    gathered_chain_ids,
    gathered_key_mask,
    input_scaling,
):
    samples, row_count, group_members, head_size = query_vectors.shape

    def absorb(running, kv_piece, key_start):
        key_count = kv_piece.shape[0]
        key_rows = kv_piece[:, :, 0].reshape(key_count, samples, group_members, head_size)
        value_rows = kv_piece[:, :, 1].reshape(key_count, samples, group_members, head_size)
        attention_logits = (
            jnp.einsum(
                "sqhd,kshd->shqk", query_vectors, key_rows, preferred_element_type=jnp.float32
            )
            * input_scaling
        )
        bias_section = per_block_bias.astype(jnp.float32)
        chain_match = (query_chain_labels[:, None] == gathered_chain_ids[None, :]).astype(
            jnp.float32
        )
        attention_logits = (
            attention_logits
            + bias_section[None]
            + chain_offset[None, :, None, None] * chain_match[None, None]
        )
        attention_logits = jnp.where(
            gathered_key_mask[None, None, None, :] > 0, attention_logits, MASKED
        )
        old_max, old_sum, old_acc = running
        new_max = jnp.maximum(old_max, jnp.max(attention_logits, axis=-1))
        unscaled = jnp.exp(attention_logits - new_max[..., None])
        new_sum = jnp.sum(unscaled, axis=-1)
        new_acc = jnp.einsum(
            "shqk,kshd->shqd",
            unscaled.astype(jnp.bfloat16),
            value_rows,
            preferred_element_type=jnp.float32,
        )
        return (new_max, new_sum, new_acc)

    return absorb


def gather_by_exchange(piece, axis_name, axis):
    count = lax.axis_size(axis_name)
    shape = piece.shape
    spread = jnp.broadcast_to(
        jnp.expand_dims(piece, axis), shape[:axis] + (count,) + shape[axis:]
    )
    joined = lax.all_to_all(spread, axis_name, axis, axis, tiled=True)
    return joined.reshape(shape[:axis] + (count * shape[axis],) + shape[axis + 1 :])


def scatter_sum_rows(partial, axis_name):
    samples, row_count, model_width = partial.shape
    count = lax.axis_size(axis_name)
    pieces = partial.reshape(samples, count, row_count // count, model_width)
    arrived = lax.all_to_all(pieces, axis_name, 1, 1, tiled=True)
    return jnp.sum(arrived.astype(jnp.float32), axis=1)


def body(
    single,
    pair_features,
    coords,
    token_centre_atom,
    chain_label,
    padding_key_mask,
    angles,
    sample_noise_level,
    centre_noise,
    embedding_weight,
    pair_bias_weight,
    same_chain_offset,
    query_key_value_gate_weight,
    attention_output_weight,
    position_update_weight,
):
    pair_normed = layer_norm(pair_features.astype(jnp.float32)).astype(jnp.bfloat16)
    local_bias = jnp.einsum(
        "ikc,cbh->bhik", pair_normed, pair_bias_weight, preferred_element_type=jnp.float32
    ).astype(jnp.bfloat16)
    column_bias = relay_bias(local_bias)
    gathered_pair_bias, first_hop = spread_bias(column_bias)
    coords, single, _ = lax.optimization_barrier((coords, single, first_hop))
    noisy = noisy_centres(coords, token_centre_atom, angles, sample_noise_level, centre_noise)
    hidden_activity = embed_tokens(single, noisy, sample_noise_level, embedding_weight)
    samples, row_count, model_width = hidden_activity.shape
    col_count = lax.axis_size("col")
    own_rows = row_count // col_count
    own_start = lax.axis_index("col") * own_rows
    own_hidden = lax.dynamic_slice_in_dim(hidden_activity, own_start, own_rows, 1)
    normed = layer_norm(hidden_activity.astype(jnp.float32)).astype(jnp.bfloat16)
    group_members = gathered_pair_bias.shape[1]
    head_size = query_key_value_gate_weight.shape[2] // group_members
    group_offset = lax.axis_index("col") * group_members
    input_scaling = head_size ** (-0.5)
    block_count = query_key_value_gate_weight.shape[0]
    for block_index in range(block_count):
        front = jnp.einsum(
            "snd,fed->fsne",
            normed,
            query_key_value_gate_weight[block_index, 0:2],
            preferred_element_type=jnp.float32,
        )
        key_value = jnp.einsum(
            "snd,fed->nsfe",
            normed,
            query_key_value_gate_weight[block_index, 2:4],
            preferred_element_type=jnp.float32,
        ).astype(jnp.bfloat16)
        if block_index == 0:
            key_marks = jnp.stack([chain_label, padding_key_mask], axis=-1).astype(jnp.bfloat16)
            key_marks = jnp.broadcast_to(key_marks[:, None, :, None], (row_count, samples, 2, 1))
            key_marks = jnp.pad(key_marks, ((0, 0), (0, 0), (0, 0), (0, 7)))
            key_value = jnp.concatenate([key_value, key_marks], axis=3)
            key_value, _ = lax.optimization_barrier((key_value, column_bias))
        gathered_key_value = gather_by_exchange(key_value, "row", 0)
        if block_index == 0:
            width = head_size * group_members
            gathered_marks = gathered_key_value[:, 0, :, width].astype(jnp.int32)
            gathered_chain_ids, gathered_key_mask = gathered_marks[:, 0], gathered_marks[:, 1]
            gathered_key_value = gathered_key_value[..., 0:width]
        query_vectors = (
            front[0].astype(jnp.bfloat16).reshape(samples, row_count, group_members, head_size)
        )
        chain_offset = lax.dynamic_slice_in_dim(
            same_chain_offset[block_index], group_offset, group_members, 0
        )
        absorb = build_absorber(
            query_vectors,
            gathered_pair_bias[block_index],
            chain_offset,
            chain_label,
            gathered_chain_ids,
            gathered_key_mask,
            input_scaling,
        )
        start_state = (
            jnp.full((samples, group_members, row_count), LOWEST, jnp.float32),
            jnp.zeros((samples, group_members, row_count), jnp.float32),
            jnp.zeros((samples, group_members, row_count, head_size), jnp.float32),
        )
        final_max, final_sum, final_acc = absorb(
            start_state, gathered_key_value, jnp.int32(0)
        )
        attended = final_acc / final_sum[..., None]
        attended = jnp.transpose(attended, (0, 2, 1, 3)).reshape(
            samples, row_count, group_members * head_size
        )
        gated_output = (jax.nn.sigmoid(front[1]) * attended).astype(jnp.bfloat16)
        partial_out = jnp.einsum(
            "kxp,pj->kxj",
            gated_output,
            attention_output_weight[block_index],
            preferred_element_type=jnp.float32,
        ).astype(jnp.bfloat16)
        summed = scatter_sum_rows(partial_out, "col")
        own_hidden = (own_hidden.astype(jnp.float32) + summed).astype(jnp.bfloat16)
        if block_index + 1 < block_count:
            own_normed = layer_norm(own_hidden.astype(jnp.float32)).astype(jnp.bfloat16)
            normed = gather_by_exchange(own_normed, "col", 1)
    hidden_activity = gather_by_exchange(own_hidden, "col", 1)
    final_normed = layer_norm(hidden_activity.astype(jnp.float32)).astype(jnp.bfloat16)
    update = jnp.einsum(
        "snd,cd->scn", final_normed, position_update_weight, preferred_element_type=jnp.float32
    )
    spread_sq = 1.0 + sample_noise_level * sample_noise_level
    denoised = (
        noisy / spread_sq[:, None, None]
        + (sample_noise_level / jnp.sqrt(spread_sq))[:, None, None] * update
    )
    return (hidden_activity, denoised)


def solution(mesh):
    return jax.shard_map(
        body,
        mesh=mesh,
        in_specs=(
            P("row", None),
            P("row", ("col", "smp"), None),
            P(),
            P("row"),
            P("row"),
            P("row"),
            P("smp", None),
            P("smp"),
            P("smp", None, "row"),
            P(),
            P(),
            P(),
            P(None, None, "col", None),
            P(None, "col", None),
            P(),
        ),
        out_specs=(P("smp", "row", None), P("smp", None, "row")),
        check_vma=False,
    )
```

```python
import jax
import jax.numpy as jnp
from jax import lax
from jax.sharding import PartitionSpec as P

EPSILON = 1e-05
MASKED = -1000000000.0
LOWEST = -1e30


def layer_norm(inputs):
    average = jnp.mean(inputs, axis=-1, keepdims=True)
    centred = inputs - average
    spread = jnp.mean(centred * centred, axis=-1, keepdims=True)
    return centred * lax.rsqrt(spread + EPSILON)


def rotation_rows(angles):
    cos_a = jnp.cos(angles[:, 0])
    sin_a = jnp.sin(angles[:, 0])
    cos_b = jnp.cos(angles[:, 1])
    sin_b = jnp.sin(angles[:, 1])
    cos_c = jnp.cos(angles[:, 2])
    sin_c = jnp.sin(angles[:, 2])
    first = jnp.stack(
        [
            cos_a * cos_b,
            cos_a * sin_b * sin_c - sin_a * cos_c,
            cos_a * sin_b * cos_c + sin_a * sin_c,
        ],
        axis=-1,
    )
    second = jnp.stack(
        [
            sin_a * cos_b,
            sin_a * sin_b * sin_c + cos_a * cos_c,
            sin_a * sin_b * cos_c - cos_a * sin_c,
        ],
        axis=-1,
    )
    third = jnp.stack([-sin_b, cos_b * sin_c, cos_b * cos_c], axis=-1)
    return jnp.stack([first, second, third], axis=1)


def noisy_centres(coords, token_centre_atom, angles, sample_noise_level, centre_noise):
    centre = jnp.take(coords, token_centre_atom, axis=1)
    rotation = rotation_rows(angles)
    turned = rotation[:, :, 0, None] * centre[0][None, None, :]
    turned = turned + rotation[:, :, 1, None] * centre[1][None, None, :]
    turned = turned + rotation[:, :, 2, None] * centre[2][None, None, :]
    return turned + sample_noise_level[:, None, None] * centre_noise


def embed_tokens(single, noisy, sample_noise_level, embedding_weight):
    scaled = noisy / jnp.sqrt(sample_noise_level * sample_noise_level + 1.0)[:, None, None]
    log_level = 0.25 * jnp.log(sample_noise_level)
    hidden_activity = single.astype(jnp.float32)[None] + scaled[:, 0, :, None] * embedding_weight[0]
    hidden_activity = hidden_activity + scaled[:, 1, :, None] * embedding_weight[1]
    hidden_activity = hidden_activity + scaled[:, 2, :, None] * embedding_weight[2]
    hidden_activity = hidden_activity + log_level[:, None, None] * embedding_weight[3]
    return hidden_activity.astype(jnp.bfloat16)


def relay_bias(local_bias):
    blocks, total_heads, row_count, keys_dev = local_bias.shape
    col_count = lax.axis_size("col")
    group_members = total_heads // col_count
    by_group = local_bias.reshape(blocks, col_count, group_members, row_count, 1, keys_dev)
    return lax.all_to_all(by_group, "col", 1, 4, tiled=True)


def spread_bias(column_bias):
    blocks, _, group_members, row_count, col_count, keys_dev = column_bias.shape
    copies = lax.axis_size("smp")
    forward = [(i, (i + 1) % copies) for i in range(copies)]
    backward = [(i, (i - 1) % copies) for i in range(copies)]
    pieces = {0: column_bias}
    rightward, leftward = column_bias, column_bias
    for step in range(1, copies // 2 + 1):
        rightward = lax.ppermute(rightward, "smp", forward)
        pieces[-step] = rightward
        if step < copies - copies // 2:
            leftward = lax.ppermute(leftward, "smp", backward)
            pieces[step] = leftward
    offsets = sorted(pieces)
    shape = (blocks, group_members, row_count, col_count, 1, keys_dev)
    stacked = jnp.concatenate([pieces[d].reshape(shape) for d in offsets], axis=4)
    stacked = jnp.roll(stacked, lax.axis_index("smp") + offsets[0], axis=4)
    return stacked.reshape(blocks, group_members, row_count, col_count * copies * keys_dev)


def build_absorber(
    query_vectors,
    per_block_bias,
    chain_offset,
    query_chain_labels,
    gathered_chain_ids,
    gathered_key_mask,
    input_scaling,
):
    samples, row_count, group_members, head_size = query_vectors.shape

    def absorb(running, kv_piece, key_start):
        key_count = kv_piece.shape[0]
        key_rows = kv_piece[:, :, 0].reshape(key_count, samples, group_members, head_size)
        value_rows = kv_piece[:, :, 1].reshape(key_count, samples, group_members, head_size)
        attention_logits = (
            jnp.einsum(
                "sqhd,kshd->shqk", query_vectors, key_rows, preferred_element_type=jnp.float32
            )
            * input_scaling
        )
        bias_section = per_block_bias.astype(jnp.float32)
        chain_match = (query_chain_labels[:, None] == gathered_chain_ids[None, :]).astype(
            jnp.float32
        )
        attention_logits = (
            attention_logits
            + bias_section[None]
            + chain_offset[None, :, None, None] * chain_match[None, None]
        )
        attention_logits = jnp.where(
            gathered_key_mask[None, None, None, :] > 0, attention_logits, MASKED
        )
        old_max, old_sum, old_acc = running
        new_max = jnp.maximum(old_max, jnp.max(attention_logits, axis=-1))
        unscaled = jnp.exp(attention_logits - new_max[..., None])
        new_sum = jnp.sum(unscaled, axis=-1)
        new_acc = jnp.einsum(
            "shqk,kshd->shqd",
            unscaled.astype(jnp.bfloat16),
            value_rows,
            preferred_element_type=jnp.float32,
        )
        return (new_max, new_sum, new_acc)

    return absorb


def gather_by_exchange(piece, axis_name, axis):
    count = lax.axis_size(axis_name)
    shape = piece.shape
    spread = jnp.broadcast_to(
        jnp.expand_dims(piece, axis), shape[:axis] + (count,) + shape[axis:]
    )
    joined = lax.all_to_all(spread, axis_name, axis, axis, tiled=True)
    return joined.reshape(shape[:axis] + (count * shape[axis],) + shape[axis + 1 :])


def scatter_sum_rows(partial, axis_name):
    samples, row_count, model_width = partial.shape
    count = lax.axis_size(axis_name)
    pieces = partial.reshape(samples, count, row_count // count, model_width)
    arrived = lax.all_to_all(pieces, axis_name, 1, 1, tiled=True)
    return jnp.sum(arrived.astype(jnp.float32), axis=1)


def body(
    single,
    pair_features,
    coords,
    token_centre_atom,
    chain_label,
    padding_key_mask,
    angles,
    sample_noise_level,
    centre_noise,
    embedding_weight,
    pair_bias_weight,
    same_chain_offset,
    query_key_value_gate_weight,
    attention_output_weight,
    position_update_weight,
):
    noisy = noisy_centres(coords, token_centre_atom, angles, sample_noise_level, centre_noise)
    hidden_activity = embed_tokens(single, noisy, sample_noise_level, embedding_weight)
    pair_normed = layer_norm(pair_features.astype(jnp.float32)).astype(jnp.bfloat16)
    local_bias = jnp.einsum(
        "ikc,cbh->bhik", pair_normed, pair_bias_weight, preferred_element_type=jnp.float32
    ).astype(jnp.bfloat16)
    column_bias = relay_bias(local_bias)
    gathered_pair_bias = spread_bias(column_bias)
    samples, row_count, model_width = hidden_activity.shape
    col_count = lax.axis_size("col")
    own_rows = row_count // col_count
    own_start = lax.axis_index("col") * own_rows
    own_hidden = lax.dynamic_slice_in_dim(hidden_activity, own_start, own_rows, 1)
    normed = layer_norm(hidden_activity.astype(jnp.float32)).astype(jnp.bfloat16)
    group_members = gathered_pair_bias.shape[1]
    head_size = query_key_value_gate_weight.shape[2] // group_members
    group_offset = lax.axis_index("col") * group_members
    input_scaling = head_size ** (-0.5)
    block_count = query_key_value_gate_weight.shape[0]
    for block_index in range(block_count):
        front = jnp.einsum(
            "snd,fed->fsne",
            normed,
            query_key_value_gate_weight[block_index, 0:2],
            preferred_element_type=jnp.float32,
        )
        key_value = jnp.einsum(
            "snd,fed->nsfe",
            normed,
            query_key_value_gate_weight[block_index, 2:4],
            preferred_element_type=jnp.float32,
        ).astype(jnp.bfloat16)
        if block_index == 0:
            key_marks = jnp.stack([chain_label, padding_key_mask], axis=-1).astype(jnp.bfloat16)
            key_marks = jnp.broadcast_to(key_marks[:, None, :, None], (row_count, samples, 2, 1))
            key_marks = jnp.pad(key_marks, ((0, 0), (0, 0), (0, 0), (0, 7)))
            key_value = jnp.concatenate([key_value, key_marks], axis=3)
            key_value, _ = lax.optimization_barrier((key_value, column_bias))
        gathered_key_value = gather_by_exchange(key_value, "row", 0)
        if block_index == 0:
            width = head_size * group_members
            gathered_marks = gathered_key_value[:, 0, :, width].astype(jnp.int32)
            gathered_chain_ids, gathered_key_mask = gathered_marks[:, 0], gathered_marks[:, 1]
            gathered_key_value = gathered_key_value[..., 0:width]
        query_vectors = (
            front[0].astype(jnp.bfloat16).reshape(samples, row_count, group_members, head_size)
        )
        chain_offset = lax.dynamic_slice_in_dim(
            same_chain_offset[block_index], group_offset, group_members, 0
        )
        absorb = build_absorber(
            query_vectors,
            gathered_pair_bias[block_index],
            chain_offset,
            chain_label,
            gathered_chain_ids,
            gathered_key_mask,
            input_scaling,
        )
        start_state = (
            jnp.full((samples, group_members, row_count), LOWEST, jnp.float32),
            jnp.zeros((samples, group_members, row_count), jnp.float32),
            jnp.zeros((samples, group_members, row_count, head_size), jnp.float32),
        )
        final_max, final_sum, final_acc = absorb(
            start_state, gathered_key_value, jnp.int32(0)
        )
        attended = final_acc / final_sum[..., None]
        attended = jnp.transpose(attended, (0, 2, 1, 3)).reshape(
            samples, row_count, group_members * head_size
        )
        gated_output = (jax.nn.sigmoid(front[1]) * attended).astype(jnp.bfloat16)
        partial_out = jnp.einsum(
            "kxp,pj->kxj",
            gated_output,
            attention_output_weight[block_index],
            preferred_element_type=jnp.float32,
        ).astype(jnp.bfloat16)
        summed = scatter_sum_rows(partial_out, "col")
        own_hidden = (own_hidden.astype(jnp.float32) + summed).astype(jnp.bfloat16)
        if block_index + 1 < block_count:
            own_normed = layer_norm(own_hidden.astype(jnp.float32)).astype(jnp.bfloat16)
            normed = gather_by_exchange(own_normed, "col", 1)
    hidden_activity = gather_by_exchange(own_hidden, "col", 1)
    final_normed = layer_norm(hidden_activity.astype(jnp.float32)).astype(jnp.bfloat16)
    update = jnp.einsum(
        "snd,cd->scn", final_normed, position_update_weight, preferred_element_type=jnp.float32
    )
    spread_sq = 1.0 + sample_noise_level * sample_noise_level
    denoised = (
        noisy / spread_sq[:, None, None]
        + (sample_noise_level / jnp.sqrt(spread_sq))[:, None, None] * update
    )
    return (hidden_activity, denoised)


def solution(mesh):
    return jax.shard_map(
        body,
        mesh=mesh,
        in_specs=(
            P("row", None),
            P("row", ("col", "smp"), None),
            P(),
            P("row"),
            P("row"),
            P("row"),
            P("smp", None),
            P("smp"),
            P("smp", None, "row"),
            P(),
            P(),
            P(),
            P(None, None, "col", None),
            P(None, "col", None),
            P(),
        ),
        out_specs=(P("smp", "row", None), P("smp", None, "row")),
        check_vma=False,
    )
```

```python
import jax
import jax.numpy as jnp
from jax import lax
from jax.sharding import PartitionSpec as P

EPSILON = 1e-05
MASKED = -1000000000.0
LOWEST = -1e30


def layer_norm(inputs):
    average = jnp.mean(inputs, axis=-1, keepdims=True)
    centred = inputs - average
    spread = jnp.mean(centred * centred, axis=-1, keepdims=True)
    return centred * lax.rsqrt(spread + EPSILON)


def rotation_rows(angles):
    cos_a = jnp.cos(angles[:, 0])
    sin_a = jnp.sin(angles[:, 0])
    cos_b = jnp.cos(angles[:, 1])
    sin_b = jnp.sin(angles[:, 1])
    cos_c = jnp.cos(angles[:, 2])
    sin_c = jnp.sin(angles[:, 2])
    first = jnp.stack(
        [
            cos_a * cos_b,
            cos_a * sin_b * sin_c - sin_a * cos_c,
            cos_a * sin_b * cos_c + sin_a * sin_c,
        ],
        axis=-1,
    )
    second = jnp.stack(
        [
            sin_a * cos_b,
            sin_a * sin_b * sin_c + cos_a * cos_c,
            sin_a * sin_b * cos_c - cos_a * sin_c,
        ],
        axis=-1,
    )
    third = jnp.stack([-sin_b, cos_b * sin_c, cos_b * cos_c], axis=-1)
    return jnp.stack([first, second, third], axis=1)


def noisy_centres(coords, token_centre_atom, angles, sample_noise_level, centre_noise):
    centre = jnp.take(coords, token_centre_atom, axis=1)
    rotation = rotation_rows(angles)
    turned = rotation[:, :, 0, None] * centre[0][None, None, :]
    turned = turned + rotation[:, :, 1, None] * centre[1][None, None, :]
    turned = turned + rotation[:, :, 2, None] * centre[2][None, None, :]
    return turned + sample_noise_level[:, None, None] * centre_noise


def embed_tokens(single, noisy, sample_noise_level, embedding_weight):
    scaled = noisy / jnp.sqrt(sample_noise_level * sample_noise_level + 1.0)[:, None, None]
    log_level = 0.25 * jnp.log(sample_noise_level)
    hidden_activity = single.astype(jnp.float32)[None] + scaled[:, 0, :, None] * embedding_weight[0]
    hidden_activity = hidden_activity + scaled[:, 1, :, None] * embedding_weight[1]
    hidden_activity = hidden_activity + scaled[:, 2, :, None] * embedding_weight[2]
    hidden_activity = hidden_activity + log_level[:, None, None] * embedding_weight[3]
    return hidden_activity.astype(jnp.bfloat16)


def relay_bias(local_bias):
    blocks, total_heads, row_count, keys_dev = local_bias.shape
    col_count = lax.axis_size("col")
    group_members = total_heads // col_count
    by_group = local_bias.reshape(blocks, col_count, group_members, row_count, 1, keys_dev)
    return lax.all_to_all(by_group, "col", 1, 4, tiled=True)


def spread_bias(column_bias):
    blocks, _, group_members, row_count, col_count, keys_dev = column_bias.shape
    copies = lax.axis_size("smp")
    forward = [(i, (i + 1) % copies) for i in range(copies)]
    backward = [(i, (i - 1) % copies) for i in range(copies)]
    pieces = {0: column_bias}
    rightward, leftward = column_bias, column_bias
    for step in range(1, copies // 2 + 1):
        rightward = lax.ppermute(rightward, "smp", forward)
        pieces[-step] = rightward
        if step < copies - copies // 2:
            leftward = lax.ppermute(leftward, "smp", backward)
            pieces[step] = leftward
    offsets = sorted(pieces)
    shape = (blocks, group_members, row_count, col_count, 1, keys_dev)
    stacked = jnp.concatenate([pieces[d].reshape(shape) for d in offsets], axis=4)
    return stacked, lax.axis_index("smp") + offsets[0]


def block_bias(stacked, shift, block_index):
    _, group_members, row_count, col_count, copies, keys_dev = stacked.shape
    rolled = jnp.roll(stacked[block_index], shift, axis=3)
    return rolled.reshape(group_members, row_count, col_count * copies * keys_dev)


def build_absorber(
    query_vectors,
    per_block_bias,
    chain_offset,
    query_chain_labels,
    gathered_chain_ids,
    gathered_key_mask,
    input_scaling,
):
    samples, row_count, group_members, head_size = query_vectors.shape

    def absorb(running, kv_piece, key_start):
        key_count = kv_piece.shape[0]
        key_rows = kv_piece[:, :, 0].reshape(key_count, samples, group_members, head_size)
        value_rows = kv_piece[:, :, 1].reshape(key_count, samples, group_members, head_size)
        attention_logits = (
            jnp.einsum(
                "sqhd,kshd->shqk", query_vectors, key_rows, preferred_element_type=jnp.float32
            )
            * input_scaling
        )
        bias_section = per_block_bias.astype(jnp.float32)
        chain_match = (query_chain_labels[:, None] == gathered_chain_ids[None, :]).astype(
            jnp.float32
        )
        attention_logits = (
            attention_logits
            + bias_section[None]
            + chain_offset[None, :, None, None] * chain_match[None, None]
        )
        attention_logits = jnp.where(
            gathered_key_mask[None, None, None, :] > 0, attention_logits, MASKED
        )
        old_max, old_sum, old_acc = running
        new_max = jnp.maximum(old_max, jnp.max(attention_logits, axis=-1))
        unscaled = jnp.exp(attention_logits - new_max[..., None])
        new_sum = jnp.sum(unscaled, axis=-1)
        new_acc = jnp.einsum(
            "shqk,kshd->shqd",
            unscaled.astype(jnp.bfloat16),
            value_rows,
            preferred_element_type=jnp.float32,
        )
        return (new_max, new_sum, new_acc)

    return absorb


def gather_by_exchange(piece, axis_name, axis):
    count = lax.axis_size(axis_name)
    shape = piece.shape
    spread = jnp.broadcast_to(
        jnp.expand_dims(piece, axis), shape[:axis] + (count,) + shape[axis:]
    )
    joined = lax.all_to_all(spread, axis_name, axis, axis, tiled=True)
    return joined.reshape(shape[:axis] + (count * shape[axis],) + shape[axis + 1 :])


def scatter_sum_rows(partial, axis_name):
    samples, row_count, model_width = partial.shape
    count = lax.axis_size(axis_name)
    pieces = partial.reshape(samples, count, row_count // count, model_width)
    arrived = lax.all_to_all(pieces, axis_name, 1, 1, tiled=True)
    return jnp.sum(arrived.astype(jnp.float32), axis=1)


def body(
    single,
    pair_features,
    coords,
    token_centre_atom,
    chain_label,
    padding_key_mask,
    angles,
    sample_noise_level,
    centre_noise,
    embedding_weight,
    pair_bias_weight,
    same_chain_offset,
    query_key_value_gate_weight,
    attention_output_weight,
    position_update_weight,
):
    noisy = noisy_centres(coords, token_centre_atom, angles, sample_noise_level, centre_noise)
    hidden_activity = embed_tokens(single, noisy, sample_noise_level, embedding_weight)
    pair_normed = layer_norm(pair_features.astype(jnp.float32)).astype(jnp.bfloat16)
    local_bias = jnp.einsum(
        "ikc,cbh->bhik", pair_normed, pair_bias_weight, preferred_element_type=jnp.float32
    ).astype(jnp.bfloat16)
    column_bias = relay_bias(local_bias)
    stacked_bias, bias_shift = spread_bias(column_bias)
    samples, row_count, model_width = hidden_activity.shape
    col_count = lax.axis_size("col")
    own_rows = row_count // col_count
    own_start = lax.axis_index("col") * own_rows
    own_hidden = lax.dynamic_slice_in_dim(hidden_activity, own_start, own_rows, 1)
    normed = layer_norm(hidden_activity.astype(jnp.float32)).astype(jnp.bfloat16)
    group_members = stacked_bias.shape[1]
    head_size = query_key_value_gate_weight.shape[2] // group_members
    group_offset = lax.axis_index("col") * group_members
    input_scaling = head_size ** (-0.5)
    block_count = query_key_value_gate_weight.shape[0]
    for block_index in range(block_count):
        front = jnp.einsum(
            "snd,fed->fsne",
            normed,
            query_key_value_gate_weight[block_index, 0:2],
            preferred_element_type=jnp.float32,
        )
        key_value = jnp.einsum(
            "snd,fed->nsfe",
            normed,
            query_key_value_gate_weight[block_index, 2:4],
            preferred_element_type=jnp.float32,
        ).astype(jnp.bfloat16)
        if block_index == 0:
            key_marks = jnp.stack([chain_label, padding_key_mask], axis=-1).astype(jnp.bfloat16)
            key_marks = jnp.broadcast_to(key_marks[:, None, :, None], (row_count, samples, 2, 1))
            key_marks = jnp.pad(key_marks, ((0, 0), (0, 0), (0, 0), (0, 7)))
            key_value = jnp.concatenate([key_value, key_marks], axis=3)
            key_value, _ = lax.optimization_barrier((key_value, column_bias))
        gathered_key_value = gather_by_exchange(key_value, "row", 0)
        if block_index == 0:
            width = head_size * group_members
            gathered_marks = gathered_key_value[:, 0, :, width].astype(jnp.int32)
            gathered_chain_ids, gathered_key_mask = gathered_marks[:, 0], gathered_marks[:, 1]
            gathered_key_value = gathered_key_value[..., 0:width]
        query_vectors = (
            front[0].astype(jnp.bfloat16).reshape(samples, row_count, group_members, head_size)
        )
        chain_offset = lax.dynamic_slice_in_dim(
            same_chain_offset[block_index], group_offset, group_members, 0
        )
        absorb = build_absorber(
            query_vectors,
            block_bias(stacked_bias, bias_shift, block_index),
            chain_offset,
            chain_label,
            gathered_chain_ids,
            gathered_key_mask,
            input_scaling,
        )
        start_state = (
            jnp.full((samples, group_members, row_count), LOWEST, jnp.float32),
            jnp.zeros((samples, group_members, row_count), jnp.float32),
            jnp.zeros((samples, group_members, row_count, head_size), jnp.float32),
        )
        final_max, final_sum, final_acc = absorb(
            start_state, gathered_key_value, jnp.int32(0)
        )
        attended = final_acc / final_sum[..., None]
        attended = jnp.transpose(attended, (0, 2, 1, 3)).reshape(
            samples, row_count, group_members * head_size
        )
        gated_output = (jax.nn.sigmoid(front[1]) * attended).astype(jnp.bfloat16)
        partial_out = jnp.einsum(
            "kxp,pj->kxj",
            gated_output,
            attention_output_weight[block_index],
            preferred_element_type=jnp.float32,
        ).astype(jnp.bfloat16)
        summed = scatter_sum_rows(partial_out, "col")
        own_hidden = (own_hidden.astype(jnp.float32) + summed).astype(jnp.bfloat16)
        if block_index + 1 < block_count:
            own_normed = layer_norm(own_hidden.astype(jnp.float32)).astype(jnp.bfloat16)
            normed = gather_by_exchange(own_normed, "col", 1)
    hidden_activity = gather_by_exchange(own_hidden, "col", 1)
    final_normed = layer_norm(hidden_activity.astype(jnp.float32)).astype(jnp.bfloat16)
    update = jnp.einsum(
        "snd,cd->scn", final_normed, position_update_weight, preferred_element_type=jnp.float32
    )
    spread_sq = 1.0 + sample_noise_level * sample_noise_level
    denoised = (
        noisy / spread_sq[:, None, None]
        + (sample_noise_level / jnp.sqrt(spread_sq))[:, None, None] * update
    )
    return (hidden_activity, denoised)


def solution(mesh):
    return jax.shard_map(
        body,
        mesh=mesh,
        in_specs=(
            P("row", None),
            P("row", ("col", "smp"), None),
            P(),
            P("row"),
            P("row"),
            P("row"),
            P("smp", None),
            P("smp"),
            P("smp", None, "row"),
            P(),
            P(),
            P(),
            P(None, None, "col", None),
            P(None, "col", None),
            P(),
        ),
        out_specs=(P("smp", "row", None), P("smp", None, "row")),
        check_vma=False,
    )
```
